128 devices in a mesh: seq: 128 (over z, x, y, core).
Axes of the slice: x: 4, y: 4, z: 4, core: 2. Of those that a mesh axis runs over, the one named last changes fastest.
Arguments:
- tokens: bfloat16 [65536, 1536], P('seq'), may hold values from -6 to 6
- norm_gain: float32 [1536], replicated, may hold values from 0.5 to 1.5
- w_query: bfloat16 [1536, 1536], replicated
- w_key_value: bfloat16 [1536, 256], replicated
- w_out: bfloat16 [1536, 1536], replicated, may hold values from -1.75 to 1.75
- segment_ids: int32 [65536], P('seq'), may hold values from 0 to 63, as said below
- page_owner: int32 [4096], P('seq'), may hold values from 0 to 127, as said below
- page_slot: int32 [4096], P('seq'), may hold values from 0 to 127, as said below
Outputs:
- attn_out: bfloat16 [65536, 1536], P('seq')
- kv_cache: bfloat16 [262144, 256], P('seq')
The draws below stay inside these ranges and needn't reach their ends.
Inputs may be any that keep to these rules, and one draw needn't show every extreme that they name: `segment_ids`: segments are contiguous runs of the stream, never falling, each of 1 to 4096 tokens; one has exactly 4096. `page_owner`: the 32 pages of one device go to different owners; some owner keeps a page of every device. `page_slot`: two pages with the same owner have different slots.
All inputs are finite; a program needn't handle non-finite values.
Results may differ from the reference program's by a relative error of at most 0.0086.
Values may be sent and summed in bfloat16 or wider, within the bound.
No kernel may reach another device: no remote copies, remote signals or barrier semaphores. Data moves between devices by JAX's collectives and lax.ppermute only.
A program may use at most 256 MiB of HBM per device.

```python
import jax
import jax.numpy as jnp
from jax import lax

D = 1536
HEADS = 12
HEAD_DIM = 128
WINDOW = 1024
MAXLEN = 4096
PAGE = 16
TOK_DEV = 512
TOKENS = 65536
DOCS = 64
PAGES = 4096
REACH = 2
CACHE_ROWS = 262144
N_SEQ = 128


def shared_key_rows(key):
    return jax.random.normal(jax.random.fold_in(key, 11), (D, HEAD_DIM), jnp.float32) * D ** (-0.5)


def draw_w_query(key, part):
    weights_all = jax.random.normal(jax.random.fold_in(key, 14), (D, HEADS, HEAD_DIM), jnp.float32) * D ** (-0.5)
    return weights_all.reshape(D, HEADS * HEAD_DIM).astype(jnp.bfloat16)


def draw_w_key_value(key, part):
    key_rows = shared_key_rows(key)
    value_rows = jax.random.normal(jax.random.fold_in(key, 16), (D, HEAD_DIM), jnp.float32) * D ** (-0.5)
    return jnp.concatenate([key_rows, value_rows], 1).astype(jnp.bfloat16)


def draw_segment_ids(key, part):
    band = MAXLEN // 4
    cut_index = jnp.arange(1, DOCS, dtype=jnp.int32)
    jitter = jax.random.randint(jax.random.fold_in(key, 41), (DOCS - 1,), 0, band)
    cuts = cut_index * band - band // 2 + jitter
    middle = N_SEQ // 2 * TOK_DEV
    middle_band = middle // band
    reach_back = min(TOK_DEV, band // 2)
    first_offset = jax.random.randint(jax.random.fold_in(key, 42), (), 1, reach_back)
    second_offset = jax.random.randint(jax.random.fold_in(key, 43), (), 1, reach_back)
    cuts = jnp.where(cut_index == middle_band, middle - reach_back + first_offset, cuts)
    cuts = jnp.where(cut_index == middle_band + 1, middle + second_offset, cuts)
    tail_start = TOKENS - 4 * band
    gaps = jax.random.randint(jax.random.fold_in(key, 44), (3,), 1, band // 8 + 1)
    cuts = jnp.where(cut_index == DOCS - 1, tail_start, cuts)
    cuts = jnp.where(cut_index == DOCS - 2, tail_start - gaps[0], cuts)
    cuts = jnp.where(cut_index == DOCS - 3, tail_start - gaps[0] - gaps[1], cuts)
    cuts = jnp.where(cut_index == DOCS - 4, tail_start - gaps[0] - gaps[1] - gaps[2], cuts)
    stream_index = jnp.arange(TOKENS, dtype=jnp.int32)
    segment_numbers = jnp.sum((stream_index[:, None] >= cuts[None, :]).astype(jnp.int32), 1)
    return segment_numbers.astype(jnp.int32)


def page_table(key):
    devices = N_SEQ
    per_device = TOK_DEV // PAGE
    busy_owner = jax.random.randint(jax.random.fold_in(key, 31), (), 0, devices)
    owner_keys = jax.random.split(jax.random.fold_in(key, 32), devices)
    others = jax.vmap(lambda subkey: jax.random.permutation(subkey, devices - 1))(owner_keys)[:, :per_device - 1] + 1
    chosen = jnp.concatenate([jnp.zeros((devices, 1), jnp.int32), others.astype(jnp.int32)], 1)
    order_keys = jax.random.split(jax.random.fold_in(key, 33), devices)
    page_order = jax.vmap(lambda subkey: jax.random.permutation(subkey, per_device))(order_keys)
    chosen = jnp.take_along_axis(chosen, page_order, 1)
    owners = (busy_owner + chosen) % devices
    slot_keys = jax.random.split(jax.random.fold_in(key, 34), devices)
    slot_perm = jax.vmap(lambda subkey: jax.random.permutation(subkey, devices))(slot_keys)
    sources = jnp.broadcast_to(jnp.arange(devices, dtype=jnp.int32)[:, None], owners.shape)
    slot_ids = slot_perm[owners, sources]
    return (owners.reshape(-1).astype(jnp.int32), slot_ids.reshape(-1).astype(jnp.int32))


def draw_page_owner(key, part):
    return page_table(key)[0]


def draw_page_slot(key, part):
    return page_table(key)[1]


def level_of(stream_key, dims, cuts, low, largest):
    loudness = 1.0
    for position, shards_of in cuts:
        draws = jax.random.uniform(jax.random.fold_in(jax.random.fold_in(stream_key, 6), position), (shards_of,), jnp.float32, low / len(cuts), largest / len(cuts))
        loudness = loudness * jnp.repeat(jnp.exp(draws), dims[position] // shards_of).reshape((-1,) + (1,) * (len(dims) - 1 - position))
    return loudness


def noise(rng, extent, spread, reach, cuts=(), kind=jnp.bfloat16):
    loudness = level_of(rng, extent, cuts, -0.22, 0.18) if cuts else 1.0
    result = jax.random.normal(rng, extent, jnp.float32) * spread * loudness
    return jnp.minimum(jnp.maximum(result, -reach), reach).astype(kind)


def setup_inputs(seed: int = 0) -> dict:
    key_of = jax.random.split(jax.random.key(seed), 9)
    tokens = noise(key_of[0], (TOKENS, D), 1.0, 6.0, ((0, 128),))
    norm_gain = jnp.clip(1.0 + 0.1 * jax.random.normal(key_of[1], (D,), jnp.float32), 0.5, 1.5)
    w_query = draw_w_query(jax.random.fold_in(key_of[8], 71), 0)
    w_key_value = draw_w_key_value(jax.random.fold_in(key_of[8], 71), 0)
    w_out = noise(key_of[4], (HEADS * HEAD_DIM, D), HEADS ** -0.5, 1.75)
    segment_ids = draw_segment_ids(jax.random.fold_in(key_of[8], 71), 0)
    page_owner = draw_page_owner(jax.random.fold_in(key_of[8], 71), 0)
    page_slot = draw_page_slot(jax.random.fold_in(key_of[8], 71), 0)
    return dict(tokens=tokens, norm_gain=norm_gain, w_query=w_query, w_key_value=w_key_value, w_out=w_out, segment_ids=segment_ids, page_owner=page_owner, page_slot=page_slot)


EPS = 1e-06
ROPE_BASE = 10000.0

def rotate(vectors, positions):
    width = vectors.shape[-1]
    half_dim = width // 2
    pair_index = jnp.arange(half_dim, dtype=jnp.float32)
    frequency = ROPE_BASE ** (-2.0 * pair_index / width)
    angles = positions.astype(jnp.float32)[:, None] * frequency[None, :]
    if vectors.ndim == 3:
        angles = angles[:, None, :]
    cosine = jnp.cos(angles)
    sine_part = jnp.sin(angles)
    first_half = vectors[..., :half_dim]
    second_half = vectors[..., half_dim:]
    return jnp.concatenate([first_half * cosine - second_half * sine_part, second_half * cosine + first_half * sine_part], -1)

def reference(tokens, norm_gain, w_query, w_key_value, w_out, segment_ids, page_owner, page_slot):
    stream_index = jnp.arange(TOKENS, dtype=jnp.int32)
    change = jnp.concatenate([jnp.ones((1,), dtype=jnp.bool_), segment_ids[1:] != segment_ids[:-1]])
    starts = lax.cummax(jnp.where(change, stream_index, 0).astype(jnp.int32))
    positions = stream_index - starts
    wide = tokens.astype(jnp.float32)
    mean_square = lax.optimization_barrier(jnp.mean(wide * wide, -1, keepdims=True))
    normed = (wide * lax.rsqrt(mean_square + EPS) * norm_gain).astype(jnp.bfloat16)
    queries = jnp.dot(normed, w_query, preferred_element_type=jnp.float32).reshape(TOKENS, HEADS, HEAD_DIM)
    queries = (rotate(queries, positions) * HEAD_DIM ** (-0.5)).astype(jnp.bfloat16)
    projected = jnp.dot(normed, w_key_value, preferred_element_type=jnp.float32)
    keyval = jnp.concatenate([rotate(projected[:, :HEAD_DIM], positions), projected[:, HEAD_DIM:]], 1).astype(jnp.bfloat16)
    padded = jnp.concatenate([jnp.zeros((REACH * TOK_DEV, 2 * HEAD_DIM), jnp.bfloat16), keyval], 0)
    span = (REACH + 1) * TOK_DEV

    def attend(block_index):
        begin = (block_index * TOK_DEV).astype(jnp.int32)
        block_queries = lax.dynamic_slice_in_dim(queries, begin, TOK_DEV, 0).astype(jnp.float32)
        block_starts = lax.dynamic_slice_in_dim(starts, begin, TOK_DEV, 0)
        key_rows = lax.dynamic_slice_in_dim(padded, begin, span, 0).astype(jnp.float32)
        query_index = begin + jnp.arange(TOK_DEV, dtype=jnp.int32)
        key_index = begin - REACH * TOK_DEV + jnp.arange(span, dtype=jnp.int32)
        valid = (key_index[None, :] >= block_starts[:, None]) & (key_index[None, :] <= query_index[:, None]) & (query_index[:, None] - key_index[None, :] < WINDOW)
        scores = jnp.einsum('thd,kd->thk', block_queries, key_rows[:, :HEAD_DIM])
        scores = jnp.where(valid[:, None, :], scores, -1e+30)
        row_peak = lax.optimization_barrier(jnp.max(scores, 2, keepdims=True))
        exponent = jnp.exp(scores - row_peak)
        probs = (exponent / lax.optimization_barrier(jnp.sum(exponent, 2, keepdims=True))).astype(jnp.bfloat16)
        context = jnp.einsum('thk,kd->thd', probs.astype(jnp.float32), key_rows[:, HEAD_DIM:])
        return context.astype(jnp.bfloat16).reshape(TOK_DEV, HEADS * HEAD_DIM)
    context = lax.map(attend, jnp.arange(N_SEQ, dtype=jnp.int32)).reshape(TOKENS, HEADS * HEAD_DIM)
    attn_out = jnp.dot(context, w_out, preferred_element_type=jnp.float32).astype(jnp.bfloat16)
    page_rows = keyval.reshape(PAGES, PAGE, 2 * HEAD_DIM)
    targets = (page_owner * N_SEQ + page_slot).astype(jnp.int32)
    cache = jnp.zeros((N_SEQ * N_SEQ, PAGE, 2 * HEAD_DIM), jnp.bfloat16).at[targets].set(page_rows)
    return (attn_out, cache.reshape(CACHE_ROWS, 2 * HEAD_DIM))
```

```python
import jax
import jax.numpy as jnp
from jax import lax
from jax.sharding import PartitionSpec as P

WINDOW = 1024
PAGE = 16
MAXLEN = 4096


EPS = 1e-06
ROPE_BASE = 10000.0


def passed_along(value, axis, by):
    size = lax.axis_size(axis)
    pairs = [(i, i + by) for i in range(size) if 0 <= i + by < size]
    return lax.ppermute(value, axis, pairs)


def rotate(vectors, positions):
    width = vectors.shape[-1]
    half_dim = width // 2
    pair_index = jnp.arange(half_dim, dtype=jnp.float32)
    frequency = ROPE_BASE ** (-2.0 * pair_index / width)
    angles = positions.astype(jnp.float32)[:, None] * frequency[None, :]
    if vectors.ndim == 3:
        angles = angles[:, None, :]
    cosine = jnp.cos(angles)
    sine_part = jnp.sin(angles)
    first_half = vectors[..., :half_dim]
    second_half = vectors[..., half_dim:]
    return jnp.concatenate(
        [
            first_half * cosine - second_half * sine_part,
            second_half * cosine + first_half * sine_part,
        ],
        -1,
    )


def body(tokens, norm_gain, w_query, w_key_value, w_out, segment_ids, page_owner, page_slot):
    row_count = tokens.shape[0]
    devices = lax.axis_size("seq")
    offset = lax.axis_index("seq") * row_count
    head_dim = w_key_value.shape[1] // 2
    head_count = w_query.shape[1] // head_dim
    local_index = jnp.arange(row_count, dtype=jnp.int32)
    global_index = offset + local_index
    change = jnp.concatenate([jnp.ones((1,), dtype=jnp.bool_), segment_ids[1:] != segment_ids[:-1]])
    local_start = lax.cummax(jnp.where(change, local_index, 0))
    place = lax.axis_index("seq")
    run_info = jnp.stack([segment_ids[-1], offset + local_start[-1]])
    hops = min(devices - 1, -(-MAXLEN // row_count))
    heard = [passed_along(run_info, "seq", hop) for hop in range(1, hops + 1)]
    prior_id = jnp.where(place >= 1, heard[0][0], -1)
    prior_first = offset
    for hop in range(hops, 0, -1):
        same = (place >= hop) & (heard[hop - 1][0] == prior_id)
        prior_first = jnp.where(same, jnp.minimum(prior_first, heard[hop - 1][1]), prior_first)
    starts = jnp.where(segment_ids == prior_id, prior_first, offset + local_start)
    positions = global_index - starts
    wide = tokens.astype(jnp.float32)
    mean_square = jnp.mean(wide * wide, -1, keepdims=True)
    normed = (wide * lax.rsqrt(mean_square + EPS) * norm_gain).astype(jnp.bfloat16)
    queries = jnp.dot(normed, w_query, preferred_element_type=jnp.float32).reshape(
        row_count, head_count, head_dim
    )
    queries = (rotate(queries, positions) * head_dim ** (-0.5)).astype(jnp.bfloat16)
    projected = jnp.dot(normed, w_key_value, preferred_element_type=jnp.float32)
    keyval = jnp.concatenate(
        [rotate(projected[:, :head_dim], positions), projected[:, head_dim:]], 1
    ).astype(jnp.bfloat16)
    reach = WINDOW // row_count
    blocks = [keyval]
    moving = keyval
    for hop_step in range(reach):
        moving = passed_along(moving, "seq", 1)
        blocks.append(moving)
    ordered = blocks[::-1]
    block_firsts = [offset - (reach - place) * row_count for place in range(reach + 1)]

    def block_scores(block_rows, block_first):
        key_index = block_first + local_index
        valid = (
            (key_index[None, :] >= starts[:, None])
            & (key_index[None, :] <= global_index[:, None])
            & (global_index[:, None] - key_index[None, :] < WINDOW)
        )
        scores = jnp.einsum(
            "thd,kd->thk", queries, block_rows[:, :head_dim], preferred_element_type=jnp.float32
        )
        return jnp.where(valid[:, None, :], scores, -1e30)

    pieces = [block_scores(ordered[place], block_firsts[place]) for place in range(reach + 1)]
    scores = jnp.concatenate(pieces, 2)
    row_peak = jnp.max(scores, 2, keepdims=True)
    exponent = jnp.exp(scores - row_peak)
    probs = (exponent / jnp.sum(exponent, 2, keepdims=True)).astype(jnp.bfloat16)
    all_values = jnp.concatenate([block_rows[:, head_dim:] for block_rows in ordered], 0)
    context = jnp.einsum("thk,kd->thd", probs, all_values, preferred_element_type=jnp.float32)
    context = context.astype(jnp.bfloat16).reshape(row_count, head_count * head_dim)
    attn_out = jnp.dot(context, w_out, preferred_element_type=jnp.float32).astype(jnp.bfloat16)
    page_rows = keyval.reshape(row_count // PAGE, PAGE * 2 * head_dim)
    width = page_rows.shape[1]
    slot_tag = jnp.zeros((page_rows.shape[0], 128), jnp.bfloat16).at[:, 0].set(
        (page_slot + 1).astype(jnp.bfloat16)
    )
    payload = jnp.concatenate([page_rows, slot_tag], 1)
    owner_hits = page_owner[:, None] == jnp.arange(devices, dtype=jnp.int32)[None, :]
    send_rows = jnp.einsum(
        "po,pc->oc", owner_hits.astype(jnp.bfloat16), payload, preferred_element_type=jnp.float32
    ).astype(jnp.bfloat16)
    got = lax.all_to_all(send_rows, "seq", split_axis=0, concat_axis=0, tiled=True)
    got_slots = got[:, width].astype(jnp.float32).astype(jnp.int32) - 1
    placed = got_slots[None, :] == jnp.arange(devices, dtype=jnp.int32)[:, None]
    cache = jnp.dot(
        placed.astype(jnp.bfloat16), got[:, :width], preferred_element_type=jnp.float32
    ).astype(jnp.bfloat16)
    return (attn_out, cache.reshape(devices * PAGE, 2 * head_dim))


def solution(mesh):
    placed = (P("seq", None), P(), P(), P(), P(), P("seq"), P("seq"), P("seq"))
    return jax.shard_map(
        body,
        mesh=mesh,
        in_specs=placed,
        out_specs=(P("seq", None), P("seq", None)),
        check_vma=False,
    )
```

```python
import functools

import jax
import jax.numpy as jnp
from jax import lax
from jax.sharding import PartitionSpec as P
from jax.experimental import pallas as pl
from jax.experimental.pallas import tpu as pltpu

WINDOW = 1024
PAGE = 16
MAXLEN = 4096


EPS = 1e-06
ROPE_BASE = 10000.0


def passed_along(value, axis, by):
    size = lax.axis_size(axis)
    pairs = [(i, i + by) for i in range(size) if 0 <= i + by < size]
    return lax.ppermute(value, axis, pairs)


def rotate(vectors, positions):
    width = vectors.shape[-1]
    half_dim = width // 2
    pair_index = jnp.arange(half_dim, dtype=jnp.float32)
    frequency = ROPE_BASE ** (-2.0 * pair_index / width)
    angles = positions.astype(jnp.float32)[:, None] * frequency[None, :]
    if vectors.ndim == 3:
        angles = angles[:, None, :]
    cosine = jnp.cos(angles)
    sine_part = jnp.sin(angles)
    first_half = vectors[..., :half_dim]
    second_half = vectors[..., half_dim:]
    return jnp.concatenate(
        [
            first_half * cosine - second_half * sine_part,
            second_half * cosine + first_half * sine_part,
        ],
        -1,
    )


def attend_kernel(query_ref, keyval_ref, first_ref, out_ref, *, tile, back, head_count, head_dim):
    step = pl.program_id(0)
    span = tile + WINDOW
    key_first = pl.multiple_of(step * tile + back - WINDOW, tile)
    rows = keyval_ref[pl.ds(key_first, span), :]
    keys = rows[:, :head_dim]
    values = rows[:, head_dim:]
    query_at = step * tile + lax.broadcasted_iota(jnp.int32, (tile, span), 0)
    key_at = key_first - back + lax.broadcasted_iota(jnp.int32, (tile, span), 1)
    valid = (key_at >= first_ref[...]) & (key_at <= query_at) & (query_at - key_at < WINDOW)
    for head in range(head_count):
        lanes = slice(head * head_dim, (head + 1) * head_dim)
        scores = lax.dot_general(
            query_ref[:, lanes], keys, (((1,), (1,)), ((), ())), preferred_element_type=jnp.float32
        )
        scores = jnp.where(valid, scores, -1e30)
        peak = jnp.max(scores, 1, keepdims=True)
        exponent = jnp.exp(scores - peak)
        probs = (exponent / jnp.sum(exponent, 1, keepdims=True)).astype(jnp.bfloat16)
        context = jnp.dot(probs, values, preferred_element_type=jnp.float32)
        out_ref[:, lanes] = context.astype(out_ref.dtype)


def attend(queries, keyval_rows, first_rel, back, tile=128):
    row_count, width = queries.shape
    head_dim = keyval_rows.shape[1] // 2
    kernel = functools.partial(
        attend_kernel, tile=tile, back=back, head_count=width // head_dim, head_dim=head_dim
    )
    return pl.pallas_call(
        kernel,
        grid=(row_count // tile,),
        in_specs=[
            pl.BlockSpec((tile, width), lambda i: (i, 0)),
            pl.BlockSpec(keyval_rows.shape, lambda i: (0, 0)),
            pl.BlockSpec((tile, 1), lambda i: (i, 0)),
        ],
        out_specs=pl.BlockSpec((tile, width), lambda i: (i, 0)),
        out_shape=jax.ShapeDtypeStruct((row_count, width), jnp.bfloat16),
    )(queries, keyval_rows, first_rel)


def body(tokens, norm_gain, w_query, w_key_value, w_out, segment_ids, page_owner, page_slot):
    row_count = tokens.shape[0]
    devices = lax.axis_size("seq")
    offset = lax.axis_index("seq") * row_count
    head_dim = w_key_value.shape[1] // 2
    head_count = w_query.shape[1] // head_dim
    local_index = jnp.arange(row_count, dtype=jnp.int32)
    global_index = offset + local_index
    change = jnp.concatenate([jnp.ones((1,), dtype=jnp.bool_), segment_ids[1:] != segment_ids[:-1]])
    local_start = lax.cummax(jnp.where(change, local_index, 0))
    place = lax.axis_index("seq")
    run_info = jnp.stack([segment_ids[-1], offset + local_start[-1]])
    hops = min(devices - 1, -(-MAXLEN // row_count))
    heard = [passed_along(run_info, "seq", hop) for hop in range(1, hops + 1)]
    prior_id = jnp.where(place >= 1, heard[0][0], -1)
    prior_first = offset
    for hop in range(hops, 0, -1):
        same = (place >= hop) & (heard[hop - 1][0] == prior_id)
        prior_first = jnp.where(same, jnp.minimum(prior_first, heard[hop - 1][1]), prior_first)
    starts = jnp.where(segment_ids == prior_id, prior_first, offset + local_start)
    positions = global_index - starts
    wide = tokens.astype(jnp.float32)
    mean_square = jnp.mean(wide * wide, -1, keepdims=True)
    normed = (wide * lax.rsqrt(mean_square + EPS) * norm_gain).astype(jnp.bfloat16)
    queries = jnp.dot(normed, w_query, preferred_element_type=jnp.float32).reshape(
        row_count, head_count, head_dim
    )
    queries = (rotate(queries, positions) * head_dim ** (-0.5)).astype(jnp.bfloat16)
    projected = jnp.dot(normed, w_key_value, preferred_element_type=jnp.float32)
    keyval = jnp.concatenate(
        [rotate(projected[:, :head_dim], positions), projected[:, head_dim:]], 1
    ).astype(jnp.bfloat16)
    reach = WINDOW // row_count
    blocks = [keyval]
    moving = keyval
    for hop_step in range(reach):
        moving = passed_along(moving, "seq", 1)
        blocks.append(moving)
    ordered = blocks[::-1]
    back = reach * row_count
    context = attend(
        queries.reshape(row_count, head_count * head_dim),
        jnp.concatenate(ordered, 0),
        (starts - offset)[:, None],
        back,
    )
    attn_out = jnp.dot(context, w_out, preferred_element_type=jnp.float32).astype(jnp.bfloat16)
    page_rows = keyval.reshape(row_count // PAGE, PAGE * 2 * head_dim)
    width = page_rows.shape[1]
    slot_tag = jnp.zeros((page_rows.shape[0], 128), jnp.bfloat16).at[:, 0].set(
        (page_slot + 1).astype(jnp.bfloat16)
    )
    payload = jnp.concatenate([page_rows, slot_tag], 1)
    owner_hits = page_owner[:, None] == jnp.arange(devices, dtype=jnp.int32)[None, :]
    send_rows = jnp.einsum(
        "po,pc->oc", owner_hits.astype(jnp.bfloat16), payload, preferred_element_type=jnp.float32
    ).astype(jnp.bfloat16)
    got = lax.all_to_all(send_rows, "seq", split_axis=0, concat_axis=0, tiled=True)
    got_slots = got[:, width].astype(jnp.float32).astype(jnp.int32) - 1
    placed = got_slots[None, :] == jnp.arange(devices, dtype=jnp.int32)[:, None]
    cache = jnp.dot(
        placed.astype(jnp.bfloat16), got[:, :width], preferred_element_type=jnp.float32
    ).astype(jnp.bfloat16)
    return (attn_out, cache.reshape(devices * PAGE, 2 * head_dim))


def solution(mesh):
    placed = (P("seq", None), P(), P(), P(), P(), P("seq"), P("seq"), P("seq"))
    return jax.shard_map(
        body,
        mesh=mesh,
        in_specs=placed,
        out_specs=(P("seq", None), P("seq", None)),
        check_vma=False,
    )
```

```python
import functools

import jax
import jax.numpy as jnp
from jax import lax
from jax.sharding import PartitionSpec as P
from jax.experimental import pallas as pl
from jax.experimental.pallas import tpu as pltpu

WINDOW = 1024
PAGE = 16


EPS = 1e-06
ROPE_BASE = 10000.0


def passed_along(value, axis, by):
    size = lax.axis_size(axis)
    pairs = [(i, i + by) for i in range(size) if 0 <= i + by < size]
    return lax.ppermute(value, axis, pairs)


def rotate(vectors, positions):
    width = vectors.shape[-1]
    half_dim = width // 2
    pair_index = jnp.arange(half_dim, dtype=jnp.float32)
    frequency = ROPE_BASE ** (-2.0 * pair_index / width)
    angles = positions.astype(jnp.float32)[:, None] * frequency[None, :]
    if vectors.ndim == 3:
        angles = angles[:, None, :]
    cosine = jnp.cos(angles)
    sine_part = jnp.sin(angles)
    first_half = vectors[..., :half_dim]
    second_half = vectors[..., half_dim:]
    return jnp.concatenate(
        [
            first_half * cosine - second_half * sine_part,
            second_half * cosine + first_half * sine_part,
        ],
        -1,
    )


def attend_kernel(query_ref, keyval_ref, first_ref, out_ref, *, tile, back, head_count, head_dim):
    step = pl.program_id(0)
    span = tile + WINDOW
    key_first = pl.multiple_of(step * tile + back - WINDOW, tile)
    rows = keyval_ref[pl.ds(key_first, span), :]
    keys = rows[:, :head_dim]
    values = rows[:, head_dim:]
    query_at = step * tile + lax.broadcasted_iota(jnp.int32, (tile, span), 0)
    key_at = key_first - back + lax.broadcasted_iota(jnp.int32, (tile, span), 1)
    valid = (key_at >= first_ref[...]) & (key_at <= query_at) & (query_at - key_at < WINDOW)
    for head in range(head_count):
        lanes = slice(head * head_dim, (head + 1) * head_dim)
        scores = lax.dot_general(
            query_ref[:, lanes], keys, (((1,), (1,)), ((), ())), preferred_element_type=jnp.float32
        )
        scores = jnp.where(valid, scores, -1e30)
        peak = jnp.max(scores, 1, keepdims=True)
        exponent = jnp.exp(scores - peak)
        probs = (exponent / jnp.sum(exponent, 1, keepdims=True)).astype(jnp.bfloat16)
        context = jnp.dot(probs, values, preferred_element_type=jnp.float32)
        out_ref[:, lanes] = context.astype(out_ref.dtype)


def attend(queries, keyval_rows, first_rel, back, tile=128):
    row_count, width = queries.shape
    head_dim = keyval_rows.shape[1] // 2
    kernel = functools.partial(
        attend_kernel, tile=tile, back=back, head_count=width // head_dim, head_dim=head_dim
    )
    return pl.pallas_call(
        kernel,
        grid=(row_count // tile,),
        in_specs=[
            pl.BlockSpec((tile, width), lambda i: (i, 0)),
            pl.BlockSpec(keyval_rows.shape, lambda i: (0, 0)),
            pl.BlockSpec((tile, 1), lambda i: (i, 0)),
        ],
        out_specs=pl.BlockSpec((tile, width), lambda i: (i, 0)),
        out_shape=jax.ShapeDtypeStruct((row_count, width), jnp.bfloat16),
    )(queries, keyval_rows, first_rel)


def body(tokens, norm_gain, w_query, w_key_value, w_out, segment_ids, page_owner, page_slot):
    row_count = tokens.shape[0]
    devices = lax.axis_size("seq")
    offset = lax.axis_index("seq") * row_count
    head_dim = w_key_value.shape[1] // 2
    head_count = w_query.shape[1] // head_dim
    local_index = jnp.arange(row_count, dtype=jnp.int32)
    global_index = offset + local_index
    change = jnp.concatenate([jnp.ones((1,), dtype=jnp.bool_), segment_ids[1:] != segment_ids[:-1]])
    local_start = lax.cummax(jnp.where(change, local_index, 0))
    place = lax.axis_index("seq")
    owner_hits = page_owner[:, None] == jnp.arange(devices, dtype=jnp.int32)[None, :]
    slot_to = jnp.sum(jnp.where(owner_hits, page_slot[:, None] + 1, 0), 0)
    notes = jnp.zeros((devices, 128), jnp.int32)
    notes = notes.at[:, 0].set(segment_ids[-1]).at[:, 1].set(offset + local_start[-1]).at[:, 2].set(slot_to)
    heard = lax.all_to_all(notes, "seq", split_axis=0, concat_axis=0, tiled=True)
    source = jnp.arange(devices, dtype=jnp.int32)
    prior_id = jnp.where(place >= 1, heard[jnp.maximum(place - 1, 0), 0], -1)
    earlier_same = (source < place) & (heard[:, 0] == prior_id)
    prior_first = jnp.min(jnp.where(earlier_same, heard[:, 1], offset))
    starts = jnp.where(segment_ids == prior_id, prior_first, offset + local_start)
    positions = global_index - starts
    wide = tokens.astype(jnp.float32)
    mean_square = jnp.mean(wide * wide, -1, keepdims=True)
    normed = (wide * lax.rsqrt(mean_square + EPS) * norm_gain).astype(jnp.bfloat16)
    queries = jnp.dot(normed, w_query, preferred_element_type=jnp.float32).reshape(
        row_count, head_count, head_dim
    )
    queries = (rotate(queries, positions) * head_dim ** (-0.5)).astype(jnp.bfloat16)
    projected = jnp.dot(normed, w_key_value, preferred_element_type=jnp.float32)
    keyval = jnp.concatenate(
        [rotate(projected[:, :head_dim], positions), projected[:, head_dim:]], 1
    ).astype(jnp.bfloat16)
    reach = WINDOW // row_count
    blocks = [keyval] + [passed_along(keyval, "seq", hop) for hop in range(1, reach + 1)]
    ordered = blocks[::-1]
    back = reach * row_count
    context = attend(
        queries.reshape(row_count, head_count * head_dim),
        jnp.concatenate(ordered, 0),
        (starts - offset)[:, None],
        back,
    )
    attn_out = jnp.dot(context, w_out, preferred_element_type=jnp.float32).astype(jnp.bfloat16)
    page_count = row_count // PAGE
    pages = keyval.reshape(page_count, PAGE, 2 * head_dim)
    pages = jnp.concatenate([pages, jnp.zeros((1, PAGE, 2 * head_dim), pages.dtype)], 0)
    page_index = jnp.arange(page_count, dtype=jnp.int32)[:, None]
    pick = jnp.sum(jnp.where(owner_hits, page_index, 0), 0)
    pick = jnp.where(jnp.any(owner_hits, 0), pick, page_count)
    got = lax.all_to_all(pages[pick], "seq", split_axis=0, concat_axis=0, tiled=True)
    got = jnp.concatenate([got, jnp.zeros((1, PAGE, 2 * head_dim), got.dtype)], 0)
    landed = heard[:, 2][None, :] == source[:, None] + 1
    from_source = jnp.sum(jnp.where(landed, source[None, :], 0), 1)
    from_source = jnp.where(jnp.any(landed, 1), from_source, devices)
    cache = got[from_source]
    return (attn_out, cache.reshape(devices * PAGE, 2 * head_dim))


def solution(mesh):
    placed = (P("seq", None), P(), P(), P(), P(), P("seq"), P("seq"), P("seq"))
    return jax.shard_map(
        body,
        mesh=mesh,
        in_specs=placed,
        out_specs=(P("seq", None), P("seq", None)),
        check_vma=False,
    )
```

```python
import functools

import jax
import jax.numpy as jnp
from jax import lax
from jax.sharding import PartitionSpec as P
from jax.experimental import pallas as pl
from jax.experimental.pallas import tpu as pltpu

WINDOW = 1024
PAGE = 16


EPS = 1e-06
ROPE_BASE = 10000.0


def passed_along(value, axis, by):
    size = lax.axis_size(axis)
    pairs = [(i, i + by) for i in range(size) if 0 <= i + by < size]
    return lax.ppermute(value, axis, pairs)


def rotate(vectors, positions):
    width = vectors.shape[-1]
    half_dim = width // 2
    pair_index = jnp.arange(half_dim, dtype=jnp.float32)
    frequency = ROPE_BASE ** (-2.0 * pair_index / width)
    angles = positions.astype(jnp.float32)[:, None] * frequency[None, :]
    if vectors.ndim == 3:
        angles = angles[:, None, :]
    cosine = jnp.cos(angles)
    sine_part = jnp.sin(angles)
    first_half = vectors[..., :half_dim]
    second_half = vectors[..., half_dim:]
    return jnp.concatenate(
        [
            first_half * cosine - second_half * sine_part,
            second_half * cosine + first_half * sine_part,
        ],
        -1,
    )


def attend_kernel(query_ref, keys_ref, values_ref, first_ref, out_ref, *, tile, back, head_count, head_dim):
    step = pl.program_id(0)
    span = tile + WINDOW
    key_first = pl.multiple_of(step * tile + back - WINDOW, tile)
    keys = keys_ref[:, pl.ds(key_first, span)]
    values = values_ref[pl.ds(key_first, span), :]
    query_at = step * tile + lax.broadcasted_iota(jnp.int32, (tile, span), 0)
    key_at = key_first - back + lax.broadcasted_iota(jnp.int32, (tile, span), 1)
    valid = (key_at >= first_ref[...]) & (key_at <= query_at) & (query_at - key_at < WINDOW)
    for head in range(head_count):
        lanes = slice(head * head_dim, (head + 1) * head_dim)
        scores = jnp.dot(query_ref[:, lanes], keys, preferred_element_type=jnp.float32)
        scores = jnp.where(valid, scores, -1e30)
        peak = jnp.max(scores, 1, keepdims=True)
        exponent = jnp.exp(scores - peak)
        probs = (exponent * (1.0 / jnp.sum(exponent, 1, keepdims=True))).astype(jnp.bfloat16)
        context = jnp.dot(probs, values, preferred_element_type=jnp.float32)
        out_ref[:, lanes] = context.astype(out_ref.dtype)


def attend(queries, keyval_rows, first_rel, back, tile=128):
    row_count, width = queries.shape
    head_dim = keyval_rows.shape[1] // 2
    kernel = functools.partial(
        attend_kernel, tile=tile, back=back, head_count=width // head_dim, head_dim=head_dim
    )
    return pl.pallas_call(
        kernel,
        grid=(row_count // tile,),
        in_specs=[
            pl.BlockSpec((tile, width), lambda i: (i, 0)),
            pl.BlockSpec((head_dim, keyval_rows.shape[0]), lambda i: (0, 0)),
            pl.BlockSpec((keyval_rows.shape[0], head_dim), lambda i: (0, 0)),
            pl.BlockSpec((tile, 1), lambda i: (i, 0)),
        ],
        out_specs=pl.BlockSpec((tile, width), lambda i: (i, 0)),
        out_shape=jax.ShapeDtypeStruct((row_count, width), jnp.bfloat16),
    )(queries, keyval_rows[:, :head_dim].T, keyval_rows[:, head_dim:], first_rel)


def body(tokens, norm_gain, w_query, w_key_value, w_out, segment_ids, page_owner, page_slot):
    row_count = tokens.shape[0]
    devices = lax.axis_size("seq")
    offset = lax.axis_index("seq") * row_count
    head_dim = w_key_value.shape[1] // 2
    head_count = w_query.shape[1] // head_dim
    local_index = jnp.arange(row_count, dtype=jnp.int32)
    global_index = offset + local_index
    change = jnp.concatenate([jnp.ones((1,), dtype=jnp.bool_), segment_ids[1:] != segment_ids[:-1]])
    local_start = lax.cummax(jnp.where(change, local_index, 0))
    place = lax.axis_index("seq")
    owner_hits = page_owner[:, None] == jnp.arange(devices, dtype=jnp.int32)[None, :]
    slot_to = jnp.sum(jnp.where(owner_hits, page_slot[:, None] + 1, 0), 0)
    notes = jnp.zeros((devices, 128), jnp.int32)
    notes = notes.at[:, 0].set(segment_ids[-1]).at[:, 1].set(offset + local_start[-1]).at[:, 2].set(slot_to)
    heard = lax.all_to_all(notes, "seq", split_axis=0, concat_axis=0, tiled=True)
    source = jnp.arange(devices, dtype=jnp.int32)
    prior_id = jnp.where(place >= 1, heard[jnp.maximum(place - 1, 0), 0], -1)
    earlier_same = (source < place) & (heard[:, 0] == prior_id)
    prior_first = jnp.min(jnp.where(earlier_same, heard[:, 1], offset))
    starts = jnp.where(segment_ids == prior_id, prior_first, offset + local_start)
    positions = global_index - starts
    wide = tokens.astype(jnp.float32)
    mean_square = jnp.mean(wide * wide, -1, keepdims=True)
    normed = (wide * lax.rsqrt(mean_square + EPS) * norm_gain).astype(jnp.bfloat16)
    queries = jnp.dot(normed, w_query, preferred_element_type=jnp.float32).reshape(
        row_count, head_count, head_dim
    )
    queries = (rotate(queries, positions) * head_dim ** (-0.5)).astype(jnp.bfloat16)
    projected = jnp.dot(normed, w_key_value, preferred_element_type=jnp.float32)
    keyval = jnp.concatenate(
        [rotate(projected[:, :head_dim], positions), projected[:, head_dim:]], 1
    ).astype(jnp.bfloat16)
    reach = WINDOW // row_count
    blocks = [keyval] + [passed_along(keyval, "seq", hop) for hop in range(1, reach + 1)]
    ordered = blocks[::-1]
    back = reach * row_count
    context = attend(
        queries.reshape(row_count, head_count * head_dim),
        jnp.concatenate(ordered, 0),
        (starts - offset)[:, None],
        back,
    )
    attn_out = jnp.dot(context, w_out, preferred_element_type=jnp.float32).astype(jnp.bfloat16)
    page_count = row_count // PAGE
    pages = keyval.reshape(page_count, PAGE, 2 * head_dim)
    pages = jnp.concatenate([pages, jnp.zeros((1, PAGE, 2 * head_dim), pages.dtype)], 0)
    page_index = jnp.arange(page_count, dtype=jnp.int32)[:, None]
    pick = jnp.sum(jnp.where(owner_hits, page_index, 0), 0)
    pick = jnp.where(jnp.any(owner_hits, 0), pick, page_count)
    got = lax.all_to_all(pages[pick], "seq", split_axis=0, concat_axis=0, tiled=True)
    got = jnp.concatenate([got, jnp.zeros((1, PAGE, 2 * head_dim), got.dtype)], 0)
    landed = heard[:, 2][None, :] == source[:, None] + 1
    from_source = jnp.sum(jnp.where(landed, source[None, :], 0), 1)
    from_source = jnp.where(jnp.any(landed, 1), from_source, devices)
    cache = got[from_source]
    return (attn_out, cache.reshape(devices * PAGE, 2 * head_dim))


def solution(mesh):
    placed = (P("seq", None), P(), P(), P(), P(), P("seq"), P("seq"), P("seq"))
    return jax.shard_map(
        body,
        mesh=mesh,
        in_specs=placed,
        out_specs=(P("seq", None), P("seq", None)),
        check_vma=False,
    )
```

```python
import functools

import jax
import jax.numpy as jnp
from jax import lax
from jax.sharding import PartitionSpec as P
from jax.experimental import pallas as pl
from jax.experimental.pallas import tpu as pltpu

WINDOW = 1024
PAGE = 16


EPS = 1e-06
ROPE_BASE = 10000.0


def passed_along(value, axis, by):
    size = lax.axis_size(axis)
    pairs = [(i, i + by) for i in range(size) if 0 <= i + by < size]
    return lax.ppermute(value, axis, pairs)


def rotate(vectors, positions):
    width = vectors.shape[-1]
    half_dim = width // 2
    pair_index = jnp.arange(half_dim, dtype=jnp.float32)
    frequency = ROPE_BASE ** (-2.0 * pair_index / width)
    angles = positions.astype(jnp.float32)[:, None] * frequency[None, :]
    if vectors.ndim == 3:
        angles = angles[:, None, :]
    cosine = jnp.cos(angles)
    sine_part = jnp.sin(angles)
    first_half = vectors[..., :half_dim]
    second_half = vectors[..., half_dim:]
    return jnp.concatenate(
        [
            first_half * cosine - second_half * sine_part,
            second_half * cosine + first_half * sine_part,
        ],
        -1,
    )


def attend_kernel(query_ref, keyval_ref, first_ref, out_ref, *, tile, back, head_count, head_dim):
    step = pl.program_id(0)
    span = tile + WINDOW
    key_first = pl.multiple_of(step * tile + back - WINDOW, tile)
    rows = keyval_ref[pl.ds(key_first, span), :]
    keys = rows[:, :head_dim]
    values = rows[:, head_dim:]
    query_at = step * tile + lax.broadcasted_iota(jnp.int32, (tile, span), 0)
    key_at = key_first - back + lax.broadcasted_iota(jnp.int32, (tile, span), 1)
    valid = (key_at >= first_ref[...]) & (key_at <= query_at) & (query_at - key_at < WINDOW)
    stacked = jnp.concatenate(
        [query_ref[:, head * head_dim : (head + 1) * head_dim] for head in range(head_count)], 0
    )
    scores = lax.dot_general(
        stacked, keys, (((1,), (1,)), ((), ())), preferred_element_type=jnp.float32
    ).reshape(head_count, tile, span)
    scores = jnp.where(valid[None], scores, -1e30)
    peak = jnp.max(scores, 2, keepdims=True)
    exponent = jnp.exp(scores - peak)
    probs = (exponent / jnp.sum(exponent, 2, keepdims=True)).astype(jnp.bfloat16)
    context = jnp.dot(
        probs.reshape(head_count * tile, span), values, preferred_element_type=jnp.float32
    )
    for head in range(head_count):
        out_ref[:, head * head_dim : (head + 1) * head_dim] = context[
            head * tile : (head + 1) * tile
        ].astype(out_ref.dtype)


def attend(queries, keyval_rows, first_rel, back, tile=128):
    row_count, width = queries.shape
    head_dim = keyval_rows.shape[1] // 2
    kernel = functools.partial(
        attend_kernel,
        tile=tile,
        back=back,
        head_count=width // head_dim,
        head_dim=head_dim,
    )
    return pl.pallas_call(
        kernel,
        grid=(row_count // tile,),
        in_specs=[
            pl.BlockSpec((tile, width), lambda i: (i, 0)),
            pl.BlockSpec(keyval_rows.shape, lambda i: (0, 0)),
            pl.BlockSpec((tile, 1), lambda i: (i, 0)),
        ],
        out_specs=pl.BlockSpec((tile, width), lambda i: (i, 0)),
        out_shape=jax.ShapeDtypeStruct((row_count, width), jnp.bfloat16),
        compiler_params=pltpu.CompilerParams(vmem_limit_bytes=60 * 1024 * 1024),
    )(queries, keyval_rows, first_rel)


def body(tokens, norm_gain, w_query, w_key_value, w_out, segment_ids, page_owner, page_slot):
    row_count = tokens.shape[0]
    devices = lax.axis_size("seq")
    offset = lax.axis_index("seq") * row_count
    head_dim = w_key_value.shape[1] // 2
    head_count = w_query.shape[1] // head_dim
    local_index = jnp.arange(row_count, dtype=jnp.int32)
    global_index = offset + local_index
    change = jnp.concatenate([jnp.ones((1,), dtype=jnp.bool_), segment_ids[1:] != segment_ids[:-1]])
    local_start = lax.cummax(jnp.where(change, local_index, 0))
    place = lax.axis_index("seq")
    owner_hits = page_owner[:, None] == jnp.arange(devices, dtype=jnp.int32)[None, :]
    slot_to = jnp.sum(jnp.where(owner_hits, page_slot[:, None] + 1, 0), 0)
    notes = jnp.zeros((devices, 128), jnp.int32)
    notes = notes.at[:, 0].set(segment_ids[-1]).at[:, 1].set(offset + local_start[-1]).at[:, 2].set(slot_to)
    heard = lax.all_to_all(notes, "seq", split_axis=0, concat_axis=0, tiled=True)
    source = jnp.arange(devices, dtype=jnp.int32)
    prior_id = jnp.where(place >= 1, heard[jnp.maximum(place - 1, 0), 0], -1)
    earlier_same = (source < place) & (heard[:, 0] == prior_id)
    prior_first = jnp.min(jnp.where(earlier_same, heard[:, 1], offset))
    starts = jnp.where(segment_ids == prior_id, prior_first, offset + local_start)
    positions = global_index - starts
    wide = tokens.astype(jnp.float32)
    mean_square = jnp.mean(wide * wide, -1, keepdims=True)
    normed = (wide * lax.rsqrt(mean_square + EPS) * norm_gain).astype(jnp.bfloat16)
    queries = jnp.dot(normed, w_query, preferred_element_type=jnp.float32).reshape(
        row_count, head_count, head_dim
    )
    queries = (rotate(queries, positions) * head_dim ** (-0.5)).astype(jnp.bfloat16)
    projected = jnp.dot(normed, w_key_value, preferred_element_type=jnp.float32)
    keyval = jnp.concatenate(
        [rotate(projected[:, :head_dim], positions), projected[:, head_dim:]], 1
    ).astype(jnp.bfloat16)
    reach = WINDOW // row_count
    blocks = [keyval] + [passed_along(keyval, "seq", hop) for hop in range(1, reach + 1)]
    ordered = blocks[::-1]
    back = reach * row_count
    context = attend(
        queries.reshape(row_count, head_count * head_dim),
        jnp.concatenate(ordered, 0),
        (starts - offset)[:, None],
        back,
    )
    attn_out = jnp.dot(context, w_out, preferred_element_type=jnp.float32).astype(jnp.bfloat16)
    page_count = row_count // PAGE
    pages = keyval.reshape(page_count, PAGE, 2 * head_dim)
    pages = jnp.concatenate([pages, jnp.zeros((1, PAGE, 2 * head_dim), pages.dtype)], 0)
    page_index = jnp.arange(page_count, dtype=jnp.int32)[:, None]
    pick = jnp.sum(jnp.where(owner_hits, page_index, 0), 0)
    pick = jnp.where(jnp.any(owner_hits, 0), pick, page_count)
    got = lax.all_to_all(pages[pick], "seq", split_axis=0, concat_axis=0, tiled=True)
    got = jnp.concatenate([got, jnp.zeros((1, PAGE, 2 * head_dim), got.dtype)], 0)
    landed = heard[:, 2][None, :] == source[:, None] + 1
    from_source = jnp.sum(jnp.where(landed, source[None, :], 0), 1)
    from_source = jnp.where(jnp.any(landed, 1), from_source, devices)
    cache = got[from_source]
    return (attn_out, cache.reshape(devices * PAGE, 2 * head_dim))


def solution(mesh):
    placed = (P("seq", None), P(), P(), P(), P(), P("seq"), P("seq"), P("seq"))
    return jax.shard_map(
        body,
        mesh=mesh,
        in_specs=placed,
        out_specs=(P("seq", None), P("seq", None)),
        check_vma=False,
    )
```

```python
import functools

import jax
import jax.numpy as jnp
from jax import lax
from jax.sharding import PartitionSpec as P
from jax.experimental import pallas as pl
from jax.experimental.pallas import tpu as pltpu

WINDOW = 1024
PAGE = 16


EPS = 1e-06
ROPE_BASE = 10000.0


def passed_along(value, axis, by):
    size = lax.axis_size(axis)
    pairs = [(i, i + by) for i in range(size) if 0 <= i + by < size]
    return lax.ppermute(value, axis, pairs)


def rotate(vectors, positions):
    width = vectors.shape[-1]
    half_dim = width // 2
    pair_index = jnp.arange(half_dim, dtype=jnp.float32)
    frequency = ROPE_BASE ** (-2.0 * pair_index / width)
    angles = positions.astype(jnp.float32)[:, None] * frequency[None, :]
    if vectors.ndim == 3:
        angles = angles[:, None, :]
    cosine = jnp.cos(angles)
    sine_part = jnp.sin(angles)
    first_half = vectors[..., :half_dim]
    second_half = vectors[..., half_dim:]
    return jnp.concatenate(
        [
            first_half * cosine - second_half * sine_part,
            second_half * cosine + first_half * sine_part,
        ],
        -1,
    )


def rotate_lanes(vectors, positions, width):
    half_dim = width // 2
    pair_index = jnp.arange(half_dim, dtype=jnp.float32)
    frequency = ROPE_BASE ** (-2.0 * pair_index / width)
    angles = positions.astype(jnp.float32)[:, None] * frequency[None, :]
    cosine = jnp.cos(angles)
    sine_part = jnp.sin(angles)
    repeats = vectors.shape[1] // width
    cosine = jnp.tile(jnp.concatenate([cosine, cosine], 1), (1, repeats))
    sine_part = jnp.tile(jnp.concatenate([-sine_part, sine_part], 1), (1, repeats))
    lane = lax.broadcasted_iota(jnp.int32, vectors.shape, 1) % width
    swapped = jnp.where(
        lane < half_dim, jnp.roll(vectors, -half_dim, 1), jnp.roll(vectors, half_dim, 1)
    )
    return vectors * cosine + swapped * sine_part


def attend_kernel(query_ref, keyval_ref, first_ref, out_ref, *, tile, back, head_count, head_dim):
    step = pl.program_id(0)
    span = tile + WINDOW
    key_first = pl.multiple_of(step * tile + back - WINDOW, tile)
    rows = keyval_ref[pl.ds(key_first, span), :]
    keys = rows[:, :head_dim]
    values = rows[:, head_dim:]
    query_at = step * tile + lax.broadcasted_iota(jnp.int32, (tile, span), 0)
    key_at = key_first - back + lax.broadcasted_iota(jnp.int32, (tile, span), 1)
    valid = (key_at >= first_ref[...]) & (key_at <= query_at) & (query_at - key_at < WINDOW)
    stacked = jnp.concatenate(
        [query_ref[:, head * head_dim : (head + 1) * head_dim] for head in range(head_count)], 0
    )
    scores = lax.dot_general(
        stacked, keys, (((1,), (1,)), ((), ())), preferred_element_type=jnp.float32
    ).reshape(head_count, tile, span)
    scores = jnp.where(valid[None], scores, -1e30)
    peak = jnp.max(scores, 2, keepdims=True)
    exponent = jnp.exp(scores - peak)
    probs = (exponent * (1.0 / jnp.sum(exponent, 2, keepdims=True))).astype(jnp.bfloat16)
    context = jnp.dot(
        probs.reshape(head_count * tile, span), values, preferred_element_type=jnp.float32
    )
    for head in range(head_count):
        out_ref[:, head * head_dim : (head + 1) * head_dim] = context[
            head * tile : (head + 1) * tile
        ].astype(out_ref.dtype)


def attend(queries, keyval_rows, first_rel, back, tile=128):
    row_count, width = queries.shape
    head_dim = keyval_rows.shape[1] // 2
    kernel = functools.partial(
        attend_kernel,
        tile=tile,
        back=back,
        head_count=width // head_dim,
        head_dim=head_dim,
    )
    return pl.pallas_call(
        kernel,
        grid=(row_count // tile,),
        in_specs=[
            pl.BlockSpec((tile, width), lambda i: (i, 0)),
            pl.BlockSpec(keyval_rows.shape, lambda i: (0, 0)),
            pl.BlockSpec((tile, 1), lambda i: (i, 0)),
        ],
        out_specs=pl.BlockSpec((tile, width), lambda i: (i, 0)),
        out_shape=jax.ShapeDtypeStruct((row_count, width), jnp.bfloat16),
        compiler_params=pltpu.CompilerParams(vmem_limit_bytes=60 * 1024 * 1024),
    )(queries, keyval_rows, first_rel)


def body(tokens, norm_gain, w_query, w_key_value, w_out, segment_ids, page_owner, page_slot):
    row_count = tokens.shape[0]
    devices = lax.axis_size("seq")
    offset = lax.axis_index("seq") * row_count
    head_dim = w_key_value.shape[1] // 2
    head_count = w_query.shape[1] // head_dim
    local_index = jnp.arange(row_count, dtype=jnp.int32)
    global_index = offset + local_index
    local_start = jnp.sum((segment_ids[None, :] < segment_ids[:, None]).astype(jnp.int32), 1)
    last_first = offset + jnp.sum((segment_ids < segment_ids[-1]).astype(jnp.int32))
    place = lax.axis_index("seq")
    owner_hits = page_owner[:, None] == jnp.arange(devices, dtype=jnp.int32)[None, :]
    slot_to = jnp.sum(jnp.where(owner_hits, page_slot[:, None] + 1, 0), 0)
    column = lax.broadcasted_iota(jnp.int32, (devices, 128), 1)
    notes = jnp.where(
        column == 0,
        segment_ids[-1],
        jnp.where(column == 1, last_first, jnp.where(column == 2, slot_to[:, None], 0)),
    )
    heard = lax.all_to_all(notes, "seq", split_axis=0, concat_axis=0, tiled=True)
    source = jnp.arange(devices, dtype=jnp.int32)
    prior_id = jnp.where(place >= 1, heard[jnp.maximum(place - 1, 0), 0], -1)
    earlier_same = (source < place) & (heard[:, 0] == prior_id)
    prior_first = jnp.min(jnp.where(earlier_same, heard[:, 1], offset))
    starts = jnp.where(segment_ids == prior_id, prior_first, offset + local_start)
    positions = global_index - starts
    wide = tokens.astype(jnp.float32)
    mean_square = jnp.mean(wide * wide, -1, keepdims=True)
    normed = (wide * lax.rsqrt(mean_square + EPS) * norm_gain).astype(jnp.bfloat16)
    queries = jnp.dot(normed, w_query, preferred_element_type=jnp.float32)
    queries = (rotate_lanes(queries, positions, head_dim) * head_dim ** (-0.5)).astype(jnp.bfloat16)
    projected = jnp.dot(normed, w_key_value, preferred_element_type=jnp.float32)
    keyval = jnp.concatenate(
        [rotate(projected[:, :head_dim], positions), projected[:, head_dim:]], 1
    ).astype(jnp.bfloat16)
    reach = WINDOW // row_count
    blocks = [keyval] + [passed_along(keyval, "seq", hop) for hop in range(1, reach + 1)]
    ordered = blocks[::-1]
    back = reach * row_count
    context = attend(
        queries,
        jnp.concatenate(ordered, 0),
        (starts - offset)[:, None],
        back,
    )
    attn_out = jnp.dot(context, w_out, preferred_element_type=jnp.float32).astype(jnp.bfloat16)
    page_count = row_count // PAGE
    pages = keyval.reshape(page_count, PAGE, 2 * head_dim)
    pages = jnp.concatenate([pages, jnp.zeros((1, PAGE, 2 * head_dim), pages.dtype)], 0)
    page_index = jnp.arange(page_count, dtype=jnp.int32)[:, None]
    pick = jnp.sum(jnp.where(owner_hits, page_index, 0), 0)
    pick = jnp.where(jnp.any(owner_hits, 0), pick, page_count)
    got = lax.all_to_all(pages[pick], "seq", split_axis=0, concat_axis=0, tiled=True)
    got = jnp.concatenate([got, jnp.zeros((1, PAGE, 2 * head_dim), got.dtype)], 0)
    landed = heard[:, 2][None, :] == source[:, None] + 1
    from_source = jnp.sum(jnp.where(landed, source[None, :], 0), 1)
    from_source = jnp.where(jnp.any(landed, 1), from_source, devices)
    cache = got[from_source]
    return (attn_out, cache.reshape(devices * PAGE, 2 * head_dim))


def solution(mesh):
    placed = (P("seq", None), P(), P(), P(), P(), P("seq"), P("seq"), P("seq"))
    return jax.shard_map(
        body,
        mesh=mesh,
        in_specs=placed,
        out_specs=(P("seq", None), P("seq", None)),
        check_vma=False,
    )
```

```python
import functools

import jax
import jax.numpy as jnp
from jax import lax
from jax.sharding import PartitionSpec as P
from jax.experimental import pallas as pl
from jax.experimental.pallas import tpu as pltpu

WINDOW = 1024
PAGE = 16


EPS = 1e-06
ROPE_BASE = 10000.0


def passed_along(value, axis, by):
    size = lax.axis_size(axis)
    pairs = [(i, i + by) for i in range(size) if 0 <= i + by < size]
    return lax.ppermute(value, axis, pairs)


def rotate(vectors, positions):
    width = vectors.shape[-1]
    half_dim = width // 2
    pair_index = jnp.arange(half_dim, dtype=jnp.float32)
    frequency = ROPE_BASE ** (-2.0 * pair_index / width)
    angles = positions.astype(jnp.float32)[:, None] * frequency[None, :]
    if vectors.ndim == 3:
        angles = angles[:, None, :]
    cosine = jnp.cos(angles)
    sine_part = jnp.sin(angles)
    first_half = vectors[..., :half_dim]
    second_half = vectors[..., half_dim:]
    return jnp.concatenate(
        [
            first_half * cosine - second_half * sine_part,
            second_half * cosine + first_half * sine_part,
        ],
        -1,
    )


def attend_kernel(query_ref, keyval_ref, first_ref, out_ref, *, tile, back, head_count, head_dim):
    step = pl.program_id(0)
    span = tile + WINDOW
    key_first = pl.multiple_of(step * tile + back - WINDOW, tile)
    rows = keyval_ref[pl.ds(key_first, span), :]
    keys = rows[:, :head_dim]
    values = rows[:, head_dim:]
    query_at = step * tile + lax.broadcasted_iota(jnp.int32, (tile, span), 0)
    key_at = key_first - back + lax.broadcasted_iota(jnp.int32, (tile, span), 1)
    valid = (key_at >= first_ref[...]) & (key_at <= query_at) & (query_at - key_at < WINDOW)
    stacked = jnp.concatenate(
        [query_ref[:, head * head_dim : (head + 1) * head_dim] for head in range(head_count)], 0
    )
    scores = lax.dot_general(
        stacked, keys, (((1,), (1,)), ((), ())), preferred_element_type=jnp.float32
    ).reshape(head_count, tile, span)
    scores = jnp.where(valid[None], scores, -1e30)
    peak = jnp.max(scores, 2, keepdims=True)
    exponent = jnp.exp(scores - peak)
    probs = (exponent / jnp.sum(exponent, 2, keepdims=True)).astype(jnp.bfloat16)
    context = jnp.dot(
        probs.reshape(head_count * tile, span), values, preferred_element_type=jnp.float32
    )
    for head in range(head_count):
        out_ref[:, head * head_dim : (head + 1) * head_dim] = context[
            head * tile : (head + 1) * tile
        ].astype(out_ref.dtype)


def attend(queries, keyval_rows, first_rel, back, tile=128):
    row_count, width = queries.shape
    head_dim = keyval_rows.shape[1] // 2
    kernel = functools.partial(
        attend_kernel,
        tile=tile,
        back=back,
        head_count=width // head_dim,
        head_dim=head_dim,
    )
    return pl.pallas_call(
        kernel,
        grid=(row_count // tile,),
        in_specs=[
            pl.BlockSpec((tile, width), lambda i: (i, 0)),
            pl.BlockSpec(keyval_rows.shape, lambda i: (0, 0)),
            pl.BlockSpec((tile, 1), lambda i: (i, 0)),
        ],
        out_specs=pl.BlockSpec((tile, width), lambda i: (i, 0)),
        out_shape=jax.ShapeDtypeStruct((row_count, width), jnp.bfloat16),
        compiler_params=pltpu.CompilerParams(vmem_limit_bytes=60 * 1024 * 1024),
    )(queries, keyval_rows, first_rel)


def body(tokens, norm_gain, w_query, w_key_value, w_out, segment_ids, page_owner, page_slot):
    row_count = tokens.shape[0]
    devices = lax.axis_size("seq")
    offset = lax.axis_index("seq") * row_count
    head_dim = w_key_value.shape[1] // 2
    head_count = w_query.shape[1] // head_dim
    local_index = jnp.arange(row_count, dtype=jnp.int32)
    global_index = offset + local_index
    local_start = jnp.sum((segment_ids[None, :] < segment_ids[:, None]).astype(jnp.int32), 1)
    last_first = offset + jnp.sum((segment_ids < segment_ids[-1]).astype(jnp.int32))
    place = lax.axis_index("seq")
    owner_hits = page_owner[:, None] == jnp.arange(devices, dtype=jnp.int32)[None, :]
    slot_to = jnp.sum(jnp.where(owner_hits, page_slot[:, None] + 1, 0), 0)
    column = lax.broadcasted_iota(jnp.int32, (devices, 128), 1)
    notes = jnp.where(
        column == 0,
        segment_ids[-1],
        jnp.where(column == 1, last_first, jnp.where(column == 2, slot_to[:, None], 0)),
    )
    heard = lax.all_to_all(notes, "seq", split_axis=0, concat_axis=0, tiled=True)
    source = jnp.arange(devices, dtype=jnp.int32)
    prior_id = jnp.where(place >= 1, heard[jnp.maximum(place - 1, 0), 0], -1)
    earlier_same = (source < place) & (heard[:, 0] == prior_id)
    prior_first = jnp.min(jnp.where(earlier_same, heard[:, 1], offset))
    starts = jnp.where(segment_ids == prior_id, prior_first, offset + local_start)
    positions = global_index - starts
    wide = tokens.astype(jnp.float32)
    mean_square = jnp.mean(wide * wide, -1, keepdims=True)
    normed = (wide * lax.rsqrt(mean_square + EPS) * norm_gain).astype(jnp.bfloat16)
    queries = jnp.dot(normed, w_query, preferred_element_type=jnp.float32).reshape(
        row_count, head_count, head_dim
    )
    queries = (rotate(queries, positions) * head_dim ** (-0.5)).astype(jnp.bfloat16)
    projected = jnp.dot(normed, w_key_value, preferred_element_type=jnp.float32)
    keyval = jnp.concatenate(
        [rotate(projected[:, :head_dim], positions), projected[:, head_dim:]], 1
    ).astype(jnp.bfloat16)
    reach = WINDOW // row_count
    blocks = [keyval] + [passed_along(keyval, "seq", hop) for hop in range(1, reach + 1)]
    ordered = blocks[::-1]
    back = reach * row_count
    context = attend(
        queries.reshape(row_count, head_count * head_dim),
        jnp.concatenate(ordered, 0),
        (starts - offset)[:, None],
        back,
    )
    attn_out = jnp.dot(context, w_out, preferred_element_type=jnp.float32).astype(jnp.bfloat16)
    page_count = row_count // PAGE
    pages = keyval.reshape(page_count, PAGE, 2 * head_dim)
    pages = jnp.concatenate([pages, jnp.zeros((1, PAGE, 2 * head_dim), pages.dtype)], 0)
    page_index = jnp.arange(page_count, dtype=jnp.int32)[:, None]
    pick = jnp.sum(jnp.where(owner_hits, page_index, 0), 0)
    pick = jnp.where(jnp.any(owner_hits, 0), pick, page_count)
    got = lax.all_to_all(pages[pick], "seq", split_axis=0, concat_axis=0, tiled=True)
    got = jnp.concatenate([got, jnp.zeros((1, PAGE, 2 * head_dim), got.dtype)], 0)
    landed = heard[:, 2][None, :] == source[:, None] + 1
    from_source = jnp.sum(jnp.where(landed, source[None, :], 0), 1)
    from_source = jnp.where(jnp.any(landed, 1), from_source, devices)
    cache = got[from_source]
    return (attn_out, cache.reshape(devices * PAGE, 2 * head_dim))


def solution(mesh):
    placed = (P("seq", None), P(), P(), P(), P(), P("seq"), P("seq"), P("seq"))
    return jax.shard_map(
        body,
        mesh=mesh,
        in_specs=placed,
        out_specs=(P("seq", None), P("seq", None)),
        check_vma=False,
    )
```

```python
import functools

import jax
import jax.numpy as jnp
from jax import lax
from jax.sharding import PartitionSpec as P
from jax.experimental import pallas as pl
from jax.experimental.pallas import tpu as pltpu

WINDOW = 1024
PAGE = 16


EPS = 1e-06
ROPE_BASE = 10000.0


def passed_along(value, axis, by):
    size = lax.axis_size(axis)
    pairs = [(i, i + by) for i in range(size) if 0 <= i + by < size]
    return lax.ppermute(value, axis, pairs)


def rotate(vectors, positions):
    width = vectors.shape[-1]
    half_dim = width // 2
    pair_index = jnp.arange(half_dim, dtype=jnp.float32)
    frequency = ROPE_BASE ** (-2.0 * pair_index / width)
    angles = positions.astype(jnp.float32)[:, None] * frequency[None, :]
    if vectors.ndim == 3:
        angles = angles[:, None, :]
    cosine = jnp.cos(angles)
    sine_part = jnp.sin(angles)
    first_half = vectors[..., :half_dim]
    second_half = vectors[..., half_dim:]
    return jnp.concatenate(
        [
            first_half * cosine - second_half * sine_part,
            second_half * cosine + first_half * sine_part,
        ],
        -1,
    )


def attend_kernel(
    query_ref, keyval_ref, first_ref, weight_ref, out_ref, *, tile, back, head_count, head_dim
):
    step = pl.program_id(0)
    span = tile + WINDOW
    key_first = pl.multiple_of(step * tile + back - WINDOW, tile)
    rows = keyval_ref[pl.ds(key_first, span), :]
    keys = rows[:, :head_dim]
    values = rows[:, head_dim:]
    query_at = step * tile + lax.broadcasted_iota(jnp.int32, (tile, span), 0)
    key_at = key_first - back + lax.broadcasted_iota(jnp.int32, (tile, span), 1)
    valid = (key_at >= first_ref[...]) & (key_at <= query_at) & (query_at - key_at < WINDOW)
    stacked = jnp.concatenate(
        [query_ref[:, head * head_dim : (head + 1) * head_dim] for head in range(head_count)], 0
    )
    scores = lax.dot_general(
        stacked, keys, (((1,), (1,)), ((), ())), preferred_element_type=jnp.float32
    ).reshape(head_count, tile, span)
    scores = jnp.where(valid[None], scores, -1e30)
    peak = jnp.max(scores, 2, keepdims=True)
    exponent = jnp.exp(scores - peak)
    probs = (exponent / jnp.sum(exponent, 2, keepdims=True)).astype(jnp.bfloat16)
    context = jnp.dot(
        probs.reshape(head_count * tile, span), values, preferred_element_type=jnp.float32
    )
    context = jnp.concatenate(
        [
            context[head * tile : (head + 1) * tile].astype(jnp.bfloat16)
            for head in range(head_count)
        ],
        1,
    )
    out_ref[...] = jnp.dot(
        context, weight_ref[...], preferred_element_type=jnp.float32
    ).astype(out_ref.dtype)


def attend(queries, keyval_rows, first_rel, weight, back, tile=128):
    row_count, width = queries.shape
    head_dim = keyval_rows.shape[1] // 2
    kernel = functools.partial(
        attend_kernel,
        tile=tile,
        back=back,
        head_count=width // head_dim,
        head_dim=head_dim,
    )
    return pl.pallas_call(
        kernel,
        grid=(row_count // tile,),
        in_specs=[
            pl.BlockSpec((tile, width), lambda i: (i, 0)),
            pl.BlockSpec(keyval_rows.shape, lambda i: (0, 0)),
            pl.BlockSpec((tile, 1), lambda i: (i, 0)),
            pl.BlockSpec(weight.shape, lambda i: (0, 0)),
        ],
        out_specs=pl.BlockSpec((tile, weight.shape[1]), lambda i: (i, 0)),
        out_shape=jax.ShapeDtypeStruct((row_count, weight.shape[1]), jnp.bfloat16),
        compiler_params=pltpu.CompilerParams(vmem_limit_bytes=60 * 1024 * 1024),
    )(queries, keyval_rows, first_rel, weight)


def body(tokens, norm_gain, w_query, w_key_value, w_out, segment_ids, page_owner, page_slot):
    row_count = tokens.shape[0]
    devices = lax.axis_size("seq")
    offset = lax.axis_index("seq") * row_count
    head_dim = w_key_value.shape[1] // 2
    head_count = w_query.shape[1] // head_dim
    local_index = jnp.arange(row_count, dtype=jnp.int32)
    global_index = offset + local_index
    local_start = jnp.sum((segment_ids[None, :] < segment_ids[:, None]).astype(jnp.int32), 1)
    last_first = offset + jnp.sum((segment_ids < segment_ids[-1]).astype(jnp.int32))
    place = lax.axis_index("seq")
    owner_hits = page_owner[:, None] == jnp.arange(devices, dtype=jnp.int32)[None, :]
    slot_to = jnp.sum(jnp.where(owner_hits, page_slot[:, None] + 1, 0), 0)
    column = lax.broadcasted_iota(jnp.int32, (devices, 128), 1)
    notes = jnp.where(
        column == 0,
        segment_ids[-1],
        jnp.where(column == 1, last_first, jnp.where(column == 2, slot_to[:, None], 0)),
    )
    heard = lax.all_to_all(notes, "seq", split_axis=0, concat_axis=0, tiled=True)
    source = jnp.arange(devices, dtype=jnp.int32)
    prior_id = jnp.where(place >= 1, heard[jnp.maximum(place - 1, 0), 0], -1)
    earlier_same = (source < place) & (heard[:, 0] == prior_id)
    prior_first = jnp.min(jnp.where(earlier_same, heard[:, 1], offset))
    starts = jnp.where(segment_ids == prior_id, prior_first, offset + local_start)
    positions = global_index - starts
    wide = tokens.astype(jnp.float32)
    mean_square = jnp.mean(wide * wide, -1, keepdims=True)
    normed = (wide * lax.rsqrt(mean_square + EPS) * norm_gain).astype(jnp.bfloat16)
    queries = jnp.dot(normed, w_query, preferred_element_type=jnp.float32).reshape(
        row_count, head_count, head_dim
    )
    queries = (rotate(queries, positions) * head_dim ** (-0.5)).astype(jnp.bfloat16)
    projected = jnp.dot(normed, w_key_value, preferred_element_type=jnp.float32)
    keyval = jnp.concatenate(
        [rotate(projected[:, :head_dim], positions), projected[:, head_dim:]], 1
    ).astype(jnp.bfloat16)
    reach = WINDOW // row_count
    blocks = [keyval] + [passed_along(keyval, "seq", hop) for hop in range(1, reach + 1)]
    ordered = blocks[::-1]
    back = reach * row_count
    attn_out = attend(
        queries.reshape(row_count, head_count * head_dim),
        jnp.concatenate(ordered, 0),
        (starts - offset)[:, None],
        w_out,
        back,
    )
    page_count = row_count // PAGE
    pages = keyval.reshape(page_count, PAGE, 2 * head_dim)
    pages = jnp.concatenate([pages, jnp.zeros((1, PAGE, 2 * head_dim), pages.dtype)], 0)
    page_index = jnp.arange(page_count, dtype=jnp.int32)[:, None]
    pick = jnp.sum(jnp.where(owner_hits, page_index, 0), 0)
    pick = jnp.where(jnp.any(owner_hits, 0), pick, page_count)
    got = lax.all_to_all(pages[pick], "seq", split_axis=0, concat_axis=0, tiled=True)
    got = jnp.concatenate([got, jnp.zeros((1, PAGE, 2 * head_dim), got.dtype)], 0)
    landed = heard[:, 2][None, :] == source[:, None] + 1
    from_source = jnp.sum(jnp.where(landed, source[None, :], 0), 1)
    from_source = jnp.where(jnp.any(landed, 1), from_source, devices)
    cache = got[from_source]
    return (attn_out, cache.reshape(devices * PAGE, 2 * head_dim))


def solution(mesh):
    placed = (P("seq", None), P(), P(), P(), P(), P("seq"), P("seq"), P("seq"))
    return jax.shard_map(
        body,
        mesh=mesh,
        in_specs=placed,
        out_specs=(P("seq", None), P("seq", None)),
        check_vma=False,
    )
```

```python
import functools

import jax
import jax.numpy as jnp
from jax import lax
from jax.sharding import PartitionSpec as P
from jax.experimental import pallas as pl
from jax.experimental.pallas import tpu as pltpu

WINDOW = 1024
PAGE = 16


EPS = 1e-06
ROPE_BASE = 10000.0


def passed_along(value, axis, by):
    size = lax.axis_size(axis)
    pairs = [(i, i + by) for i in range(size) if 0 <= i + by < size]
    return lax.ppermute(value, axis, pairs)


def rotate(vectors, positions):
    width = vectors.shape[-1]
    half_dim = width // 2
    pair_index = jnp.arange(half_dim, dtype=jnp.float32)
    frequency = ROPE_BASE ** (-2.0 * pair_index / width)
    angles = positions.astype(jnp.float32)[:, None] * frequency[None, :]
    if vectors.ndim == 3:
        angles = angles[:, None, :]
    cosine = jnp.cos(angles)
    sine_part = jnp.sin(angles)
    first_half = vectors[..., :half_dim]
    second_half = vectors[..., half_dim:]
    return jnp.concatenate(
        [
            first_half * cosine - second_half * sine_part,
            second_half * cosine + first_half * sine_part,
        ],
        -1,
    )


def attend_kernel(
    query_ref,
    keyval_ref,
    first_ref,
    weight_ref,
    out_ref,
    bias_ref,
    scores_ref,
    *,
    tile,
    back,
    head_count,
    head_dim,
    chunk,
):
    step = pl.program_id(0)
    span = tile + WINDOW
    key_first = pl.multiple_of(step * tile + back - WINDOW, tile)
    rows = keyval_ref[pl.ds(key_first, span), :]
    keys = rows[:, :head_dim]
    values = rows[:, head_dim:]
    query_at = step * tile + lax.broadcasted_iota(jnp.int32, (tile, span), 0)
    key_at = key_first - back + lax.broadcasted_iota(jnp.int32, (tile, span), 1)
    valid = (key_at >= first_ref[...]) & (key_at <= query_at) & (query_at - key_at < WINDOW)
    bias_ref[...] = jnp.where(valid, 0.0, -1e30).astype(jnp.float32)
    stacked = jnp.concatenate(
        [query_ref[:, head * head_dim : (head + 1) * head_dim] for head in range(head_count)], 0
    )
    scores_ref[...] = lax.dot_general(
        stacked, keys, (((1,), (1,)), ((), ())), preferred_element_type=jnp.float32
    )

    for head in range(head_count):
        for part in range(tile // chunk):
            row = head * tile + part * chunk
            scores = scores_ref[row : row + chunk, :] + bias_ref[part * chunk : (part + 1) * chunk, :]
            peak = jnp.max(scores, 1, keepdims=True)
            exponent = jnp.exp(scores - peak)
            probs = exponent / jnp.sum(exponent, 1, keepdims=True)
            scores_ref[row : row + chunk, :] = probs
    context = jnp.dot(
        scores_ref[...].astype(jnp.bfloat16), values, preferred_element_type=jnp.float32
    )
    context = jnp.concatenate(
        [
            context[head * tile : (head + 1) * tile].astype(jnp.bfloat16)
            for head in range(head_count)
        ],
        1,
    )
    out_ref[...] = jnp.dot(
        context, weight_ref[...], preferred_element_type=jnp.float32
    ).astype(out_ref.dtype)


def attend(queries, keyval_rows, first_rel, weight, back, tile=128, chunk=32):
    row_count, width = queries.shape
    head_dim = keyval_rows.shape[1] // 2
    kernel = functools.partial(
        attend_kernel,
        tile=tile,
        back=back,
        head_count=width // head_dim,
        head_dim=head_dim,
        chunk=chunk,
    )
    return pl.pallas_call(
        kernel,
        grid=(row_count // tile,),
        in_specs=[
            pl.BlockSpec((tile, width), lambda i: (i, 0)),
            pl.BlockSpec(keyval_rows.shape, lambda i: (0, 0)),
            pl.BlockSpec((tile, 1), lambda i: (i, 0)),
            pl.BlockSpec(weight.shape, lambda i: (0, 0)),
        ],
        out_specs=pl.BlockSpec((tile, weight.shape[1]), lambda i: (i, 0)),
        out_shape=jax.ShapeDtypeStruct((row_count, weight.shape[1]), jnp.bfloat16),
        scratch_shapes=[
            pltpu.VMEM((tile, tile + WINDOW), jnp.float32),
            pltpu.VMEM((width // head_dim * tile, tile + WINDOW), jnp.float32),
        ],
        compiler_params=pltpu.CompilerParams(vmem_limit_bytes=60 * 1024 * 1024),
    )(queries, keyval_rows, first_rel, weight)


def body(tokens, norm_gain, w_query, w_key_value, w_out, segment_ids, page_owner, page_slot):
    row_count = tokens.shape[0]
    devices = lax.axis_size("seq")
    offset = lax.axis_index("seq") * row_count
    head_dim = w_key_value.shape[1] // 2
    head_count = w_query.shape[1] // head_dim
    local_index = jnp.arange(row_count, dtype=jnp.int32)
    global_index = offset + local_index
    local_start = jnp.sum((segment_ids[None, :] < segment_ids[:, None]).astype(jnp.int32), 1)
    last_first = offset + jnp.sum((segment_ids < segment_ids[-1]).astype(jnp.int32))
    place = lax.axis_index("seq")
    owner_hits = page_owner[:, None] == jnp.arange(devices, dtype=jnp.int32)[None, :]
    slot_to = jnp.sum(jnp.where(owner_hits, page_slot[:, None] + 1, 0), 0)
    column = lax.broadcasted_iota(jnp.int32, (devices, 128), 1)
    notes = jnp.where(
        column == 0,
        segment_ids[-1],
        jnp.where(column == 1, last_first, jnp.where(column == 2, slot_to[:, None], 0)),
    )
    heard = lax.all_to_all(notes, "seq", split_axis=0, concat_axis=0, tiled=True)
    source = jnp.arange(devices, dtype=jnp.int32)
    prior_id = jnp.where(place >= 1, heard[jnp.maximum(place - 1, 0), 0], -1)
    earlier_same = (source < place) & (heard[:, 0] == prior_id)
    prior_first = jnp.min(jnp.where(earlier_same, heard[:, 1], offset))
    starts = jnp.where(segment_ids == prior_id, prior_first, offset + local_start)
    positions = global_index - starts
    wide = tokens.astype(jnp.float32)
    mean_square = jnp.mean(wide * wide, -1, keepdims=True)
    normed = (wide * lax.rsqrt(mean_square + EPS) * norm_gain).astype(jnp.bfloat16)
    queries = jnp.dot(normed, w_query, preferred_element_type=jnp.float32).reshape(
        row_count, head_count, head_dim
    )
    queries = (rotate(queries, positions) * head_dim ** (-0.5)).astype(jnp.bfloat16)
    projected = jnp.dot(normed, w_key_value, preferred_element_type=jnp.float32)
    keyval = jnp.concatenate(
        [rotate(projected[:, :head_dim], positions), projected[:, head_dim:]], 1
    ).astype(jnp.bfloat16)
    reach = WINDOW // row_count
    blocks = [keyval] + [passed_along(keyval, "seq", hop) for hop in range(1, reach + 1)]
    ordered = blocks[::-1]
    back = reach * row_count
    attn_out = attend(
        queries.reshape(row_count, head_count * head_dim),
        jnp.concatenate(ordered, 0),
        (starts - offset)[:, None],
        w_out,
        back,
    )
    page_count = row_count // PAGE
    pages = keyval.reshape(page_count, PAGE, 2 * head_dim)
    pages = jnp.concatenate([pages, jnp.zeros((1, PAGE, 2 * head_dim), pages.dtype)], 0)
    page_index = jnp.arange(page_count, dtype=jnp.int32)[:, None]
    pick = jnp.sum(jnp.where(owner_hits, page_index, 0), 0)
    pick = jnp.where(jnp.any(owner_hits, 0), pick, page_count)
    got = lax.all_to_all(pages[pick], "seq", split_axis=0, concat_axis=0, tiled=True)
    got = jnp.concatenate([got, jnp.zeros((1, PAGE, 2 * head_dim), got.dtype)], 0)
    landed = heard[:, 2][None, :] == source[:, None] + 1
    from_source = jnp.sum(jnp.where(landed, source[None, :], 0), 1)
    from_source = jnp.where(jnp.any(landed, 1), from_source, devices)
    cache = got[from_source]
    return (attn_out, cache.reshape(devices * PAGE, 2 * head_dim))


def solution(mesh):
    placed = (P("seq", None), P(), P(), P(), P(), P("seq"), P("seq"), P("seq"))
    return jax.shard_map(
        body,
        mesh=mesh,
        in_specs=placed,
        out_specs=(P("seq", None), P("seq", None)),
        check_vma=False,
    )
```

```python
import functools

import jax
import jax.numpy as jnp
from jax import lax
from jax.sharding import PartitionSpec as P
from jax.experimental import pallas as pl
from jax.experimental.pallas import tpu as pltpu

WINDOW = 1024
PAGE = 16


EPS = 1e-06
ROPE_BASE = 10000.0


def passed_along(value, axis, by):
    size = lax.axis_size(axis)
    pairs = [(i, i + by) for i in range(size) if 0 <= i + by < size]
    return lax.ppermute(value, axis, pairs)


def rotate(vectors, positions):
    width = vectors.shape[-1]
    half_dim = width // 2
    pair_index = jnp.arange(half_dim, dtype=jnp.float32)
    frequency = ROPE_BASE ** (-2.0 * pair_index / width)
    angles = positions.astype(jnp.float32)[:, None] * frequency[None, :]
    if vectors.ndim == 3:
        angles = angles[:, None, :]
    cosine = jnp.cos(angles)
    sine_part = jnp.sin(angles)
    first_half = vectors[..., :half_dim]
    second_half = vectors[..., half_dim:]
    return jnp.concatenate(
        [
            first_half * cosine - second_half * sine_part,
            second_half * cosine + first_half * sine_part,
        ],
        -1,
    )


def attend_kernel(
    query_ref,
    table_ref,
    early_ref,
    middle_ref,
    own_ref,
    weight_ref,
    out_ref,
    rows_ref,
    bias_ref,
    scores_ref,
    *,
    tile,
    back,
    head_count,
    head_dim,
    chunk,
):
    step = pl.program_id(0)
    block = own_ref.shape[0]

    @pl.when(step == 0)
    def _():
        rows_ref[0:block, :] = early_ref[...]
        rows_ref[block : 2 * block, :] = middle_ref[...]
        rows_ref[2 * block : 3 * block, :] = own_ref[...]

    span = tile + WINDOW
    key_first = pl.multiple_of(step * tile + back - WINDOW, tile)
    rows = rows_ref[pl.ds(key_first, span), :]
    keys = rows[:, :head_dim]
    values = rows[:, head_dim:]
    cosine = table_ref[:, 0:head_dim]
    sine_part = table_ref[:, head_dim : 2 * head_dim]
    first = table_ref[:, 2 * head_dim : 2 * head_dim + 1].astype(jnp.int32)
    query_at = step * tile + lax.broadcasted_iota(jnp.int32, (tile, span), 0)
    key_at = key_first - back + lax.broadcasted_iota(jnp.int32, (tile, span), 1)
    valid = (key_at >= first) & (key_at <= query_at) & (query_at - key_at < WINDOW)
    bias_ref[...] = jnp.where(valid, 0.0, -1e30).astype(jnp.float32)
    pieces = []
    for head in range(head_count):
        vectors = query_ref[:, head * head_dim : (head + 1) * head_dim]
        swapped = pltpu.roll(vectors, head_dim // 2, 1)
        turned = vectors * cosine + swapped * sine_part
        pieces.append((turned * head_dim ** (-0.5)).astype(jnp.bfloat16))
    stacked = jnp.concatenate(pieces, 0)
    scores_ref[...] = lax.dot_general(
        stacked, keys, (((1,), (1,)), ((), ())), preferred_element_type=jnp.float32
    )
    for head in range(head_count):
        for part in range(tile // chunk):
            row = head * tile + part * chunk
            scores = scores_ref[row : row + chunk, :] + bias_ref[part * chunk : (part + 1) * chunk, :]
            peak = jnp.max(scores, 1, keepdims=True)
            exponent = jnp.exp(scores - peak)
            probs = exponent / jnp.sum(exponent, 1, keepdims=True)
            scores_ref[row : row + chunk, :] = probs
    context = jnp.dot(
        scores_ref[...].astype(jnp.bfloat16), values, preferred_element_type=jnp.float32
    )
    context = jnp.concatenate(
        [
            context[head * tile : (head + 1) * tile].astype(jnp.bfloat16)
            for head in range(head_count)
        ],
        1,
    )
    out_ref[...] = jnp.dot(
        context, weight_ref[...], preferred_element_type=jnp.float32
    ).astype(out_ref.dtype)


def attend(projected, table, blocks, weight, back, tile=128, chunk=32):
    row_count, width = projected.shape
    head_dim = blocks[0].shape[1] // 2
    kernel = functools.partial(
        attend_kernel,
        tile=tile,
        back=back,
        head_count=width // head_dim,
        head_dim=head_dim,
        chunk=chunk,
    )
    whole = pl.BlockSpec(blocks[0].shape, lambda i: (0, 0))
    return pl.pallas_call(
        kernel,
        grid=(row_count // tile,),
        in_specs=[
            pl.BlockSpec((tile, width), lambda i: (i, 0)),
            pl.BlockSpec((tile, table.shape[1]), lambda i: (i, 0)),
            whole,
            whole,
            whole,
            pl.BlockSpec(weight.shape, lambda i: (0, 0)),
        ],
        out_specs=pl.BlockSpec((tile, weight.shape[1]), lambda i: (i, 0)),
        out_shape=jax.ShapeDtypeStruct((row_count, weight.shape[1]), jnp.bfloat16),
        scratch_shapes=[
            pltpu.VMEM((len(blocks) * row_count, 2 * head_dim), blocks[0].dtype),
            pltpu.VMEM((tile, tile + WINDOW), jnp.float32),
            pltpu.VMEM((width // head_dim * tile, tile + WINDOW), jnp.float32),
        ],
        compiler_params=pltpu.CompilerParams(vmem_limit_bytes=60 * 1024 * 1024),
    )(projected, table, *blocks, weight)


def body(tokens, norm_gain, w_query, w_key_value, w_out, segment_ids, page_owner, page_slot):
    row_count = tokens.shape[0]
    devices = lax.axis_size("seq")
    offset = lax.axis_index("seq") * row_count
    head_dim = w_key_value.shape[1] // 2
    head_count = w_query.shape[1] // head_dim
    local_index = jnp.arange(row_count, dtype=jnp.int32)
    global_index = offset + local_index
    local_start = jnp.sum((segment_ids[None, :] < segment_ids[:, None]).astype(jnp.int32), 1)
    last_first = offset + jnp.sum((segment_ids < segment_ids[-1]).astype(jnp.int32))
    place = lax.axis_index("seq")
    owner_hits = page_owner[:, None] == jnp.arange(devices, dtype=jnp.int32)[None, :]
    slot_to = jnp.sum(jnp.where(owner_hits, page_slot[:, None] + 1, 0), 0)
    column = lax.broadcasted_iota(jnp.int32, (devices, 128), 1)
    notes = jnp.where(
        column == 0,
        segment_ids[-1],
        jnp.where(column == 1, last_first, jnp.where(column == 2, slot_to[:, None], 0)),
    )
    heard = lax.all_to_all(notes, "seq", split_axis=0, concat_axis=0, tiled=True)
    source = jnp.arange(devices, dtype=jnp.int32)
    prior_id = jnp.where(place >= 1, heard[jnp.maximum(place - 1, 0), 0], -1)
    earlier_same = (source < place) & (heard[:, 0] == prior_id)
    prior_first = jnp.min(jnp.where(earlier_same, heard[:, 1], offset))
    starts = jnp.where(segment_ids == prior_id, prior_first, offset + local_start)
    positions = global_index - starts
    wide = tokens.astype(jnp.float32)
    mean_square = jnp.mean(wide * wide, -1, keepdims=True)
    normed = (wide * lax.rsqrt(mean_square + EPS) * norm_gain).astype(jnp.bfloat16)
    queries = jnp.dot(normed, w_query, preferred_element_type=jnp.float32)
    pair_index = jnp.arange(head_dim // 2, dtype=jnp.float32)
    frequency = ROPE_BASE ** (-2.0 * pair_index / head_dim)
    angles = positions.astype(jnp.float32)[:, None] * frequency[None, :]
    table = jnp.concatenate(
        [
            jnp.cos(angles),
            jnp.cos(angles),
            -jnp.sin(angles),
            jnp.sin(angles),
            jnp.broadcast_to((starts - offset).astype(jnp.float32)[:, None], (row_count, head_dim)),
        ],
        1,
    )
    projected = jnp.dot(normed, w_key_value, preferred_element_type=jnp.float32)
    keyval = jnp.concatenate(
        [rotate(projected[:, :head_dim], positions), projected[:, head_dim:]], 1
    ).astype(jnp.bfloat16)
    reach = WINDOW // row_count
    blocks = [keyval] + [passed_along(keyval, "seq", hop) for hop in range(1, reach + 1)]
    ordered = blocks[::-1]
    attn_out = attend(queries, table, ordered, w_out, reach * row_count)
    page_count = row_count // PAGE
    pages = keyval.reshape(page_count, PAGE, 2 * head_dim)
    pages = jnp.concatenate([pages, jnp.zeros((1, PAGE, 2 * head_dim), pages.dtype)], 0)
    page_index = jnp.arange(page_count, dtype=jnp.int32)[:, None]
    pick = jnp.sum(jnp.where(owner_hits, page_index, 0), 0)
    pick = jnp.where(jnp.any(owner_hits, 0), pick, page_count)
    got = lax.all_to_all(pages[pick], "seq", split_axis=0, concat_axis=0, tiled=True)
    got = jnp.concatenate([got, jnp.zeros((1, PAGE, 2 * head_dim), got.dtype)], 0)
    landed = heard[:, 2][None, :] == source[:, None] + 1
    from_source = jnp.sum(jnp.where(landed, source[None, :], 0), 1)
    from_source = jnp.where(jnp.any(landed, 1), from_source, devices)
    cache = got[from_source]
    return (attn_out, cache.reshape(devices * PAGE, 2 * head_dim))


def solution(mesh):
    placed = (P("seq", None), P(), P(), P(), P(), P("seq"), P("seq"), P("seq"))
    return jax.shard_map(
        body,
        mesh=mesh,
        in_specs=placed,
        out_specs=(P("seq", None), P("seq", None)),
        check_vma=False,
    )
```

```python
import functools

import jax
import jax.numpy as jnp
from jax import lax
from jax.sharding import PartitionSpec as P
from jax.experimental import pallas as pl
from jax.experimental.pallas import tpu as pltpu

WINDOW = 1024
PAGE = 16


EPS = 1e-06
ROPE_BASE = 10000.0


def passed_along(value, axis, by):
    size = lax.axis_size(axis)
    pairs = [(i, i + by) for i in range(size) if 0 <= i + by < size]
    return lax.ppermute(value, axis, pairs)


def rotate(vectors, positions):
    width = vectors.shape[-1]
    half_dim = width // 2
    pair_index = jnp.arange(half_dim, dtype=jnp.float32)
    frequency = ROPE_BASE ** (-2.0 * pair_index / width)
    angles = positions.astype(jnp.float32)[:, None] * frequency[None, :]
    if vectors.ndim == 3:
        angles = angles[:, None, :]
    cosine = jnp.cos(angles)
    sine_part = jnp.sin(angles)
    first_half = vectors[..., :half_dim]
    second_half = vectors[..., half_dim:]
    return jnp.concatenate(
        [
            first_half * cosine - second_half * sine_part,
            second_half * cosine + first_half * sine_part,
        ],
        -1,
    )


def attend_kernel(
    query_ref,
    table_ref,
    early_ref,
    middle_ref,
    own_ref,
    weight_ref,
    out_ref,
    rows_ref,
    bias_ref,
    scores_ref,
    *,
    tile,
    back,
    head_count,
    head_dim,
    chunk,
):
    step = pl.program_id(0)
    block = own_ref.shape[0]

    @pl.when(step == 0)
    def _():
        rows_ref[0:block, :] = early_ref[...]
        rows_ref[block : 2 * block, :] = middle_ref[...]
        rows_ref[2 * block : 3 * block, :] = own_ref[...]

    span = tile + WINDOW
    key_first = pl.multiple_of(step * tile + back - WINDOW, tile)
    rows = rows_ref[pl.ds(key_first, span), :]
    keys = rows[:, :head_dim]
    values = rows[:, head_dim:]
    cosine = table_ref[:, 0:head_dim]
    sine_part = table_ref[:, head_dim : 2 * head_dim]
    first = table_ref[:, 2 * head_dim : 2 * head_dim + 1].astype(jnp.int32)
    query_at = step * tile + lax.broadcasted_iota(jnp.int32, (tile, span), 0)
    key_at = key_first - back + lax.broadcasted_iota(jnp.int32, (tile, span), 1)
    valid = (key_at >= first) & (key_at <= query_at) & (query_at - key_at < WINDOW)
    bias_ref[...] = jnp.where(valid, 0.0, -1e30).astype(jnp.float32)
    pieces = []
    for head in range(head_count):
        vectors = query_ref[:, head * head_dim : (head + 1) * head_dim]
        swapped = pltpu.roll(vectors, head_dim // 2, 1)
        turned = vectors * cosine + swapped * sine_part
        pieces.append((turned * head_dim ** (-0.5)).astype(jnp.bfloat16))
    stacked = jnp.concatenate(pieces, 0)
    scores_ref[...] = lax.dot_general(
        stacked, keys, (((1,), (1,)), ((), ())), preferred_element_type=jnp.float32
    )
    for head in range(head_count):
        for part in range(tile // chunk):
            row = head * tile + part * chunk
            scores = scores_ref[row : row + chunk, :] + bias_ref[part * chunk : (part + 1) * chunk, :]
            peak = jnp.max(scores, 1, keepdims=True)
            exponent = jnp.exp(scores - peak)
            probs = exponent / jnp.sum(exponent, 1, keepdims=True)
            scores_ref[row : row + chunk, :] = probs
    context = jnp.dot(
        scores_ref[...].astype(jnp.bfloat16), values, preferred_element_type=jnp.float32
    )
    context = jnp.concatenate(
        [
            context[head * tile : (head + 1) * tile].astype(jnp.bfloat16)
            for head in range(head_count)
        ],
        1,
    )
    out_ref[...] = jnp.dot(
        context, weight_ref[...], preferred_element_type=jnp.float32
    ).astype(out_ref.dtype)


def attend(projected, table, blocks, weight, back, tile=128, chunk=32):
    row_count, width = projected.shape
    head_dim = blocks[0].shape[1] // 2
    kernel = functools.partial(
        attend_kernel,
        tile=tile,
        back=back,
        head_count=width // head_dim,
        head_dim=head_dim,
        chunk=chunk,
    )
    whole = pl.BlockSpec(blocks[0].shape, lambda i: (0, 0))
    return pl.pallas_call(
        kernel,
        grid=(row_count // tile,),
        in_specs=[
            pl.BlockSpec((tile, width), lambda i: (i, 0)),
            pl.BlockSpec((tile, table.shape[1]), lambda i: (i, 0)),
            whole,
            whole,
            whole,
            pl.BlockSpec(weight.shape, lambda i: (0, 0)),
        ],
        out_specs=pl.BlockSpec((tile, weight.shape[1]), lambda i: (i, 0)),
        out_shape=jax.ShapeDtypeStruct((row_count, weight.shape[1]), jnp.bfloat16),
        scratch_shapes=[
            pltpu.VMEM((len(blocks) * row_count, 2 * head_dim), blocks[0].dtype),
            pltpu.VMEM((tile, tile + WINDOW), jnp.float32),
            pltpu.VMEM((width // head_dim * tile, tile + WINDOW), jnp.float32),
        ],
        compiler_params=pltpu.CompilerParams(vmem_limit_bytes=60 * 1024 * 1024),
    )(projected, table, *blocks, weight)


def layer(tokens, norm_gain, w_query, w_key_value, w_out, segment_ids, page_owner, page_slot):
    row_count = tokens.shape[0]
    devices = lax.axis_size("seq")
    offset = lax.axis_index("seq") * row_count
    head_dim = w_key_value.shape[1] // 2
    local_index = jnp.arange(row_count, dtype=jnp.int32)
    global_index = offset + local_index
    local_start = jnp.sum((segment_ids[None, :] < segment_ids[:, None]).astype(jnp.int32), 1)
    last_first = offset + jnp.sum((segment_ids < segment_ids[-1]).astype(jnp.int32))
    place = lax.axis_index("seq")
    owner_hits = page_owner[:, None] == jnp.arange(devices, dtype=jnp.int32)[None, :]
    slot_to = jnp.sum(jnp.where(owner_hits, page_slot[:, None] + 1, 0), 0)
    column = lax.broadcasted_iota(jnp.int32, (devices, 128), 1)
    notes = jnp.where(
        column == 0,
        segment_ids[-1],
        jnp.where(column == 1, last_first, jnp.where(column == 2, slot_to[:, None], 0)),
    )
    heard = lax.all_to_all(notes, "seq", split_axis=0, concat_axis=0, tiled=True)
    source = jnp.arange(devices, dtype=jnp.int32)
    prior_id = jnp.where(place >= 1, heard[jnp.maximum(place - 1, 0), 0], -1)
    earlier_same = (source < place) & (heard[:, 0] == prior_id)
    prior_first = jnp.min(jnp.where(earlier_same, heard[:, 1], offset))
    starts = jnp.where(segment_ids == prior_id, prior_first, offset + local_start)
    positions = global_index - starts
    wide = tokens.astype(jnp.float32)
    mean_square = jnp.mean(wide * wide, -1, keepdims=True)
    normed = (wide * lax.rsqrt(mean_square + EPS) * norm_gain).astype(jnp.bfloat16)
    queries = jnp.dot(normed, w_query, preferred_element_type=jnp.float32)
    pair_index = jnp.arange(head_dim // 2, dtype=jnp.float32)
    frequency = ROPE_BASE ** (-2.0 * pair_index / head_dim)
    angles = positions.astype(jnp.float32)[:, None] * frequency[None, :]
    table = jnp.concatenate(
        [
            jnp.cos(angles),
            jnp.cos(angles),
            -jnp.sin(angles),
            jnp.sin(angles),
            jnp.broadcast_to((starts - offset).astype(jnp.float32)[:, None], (row_count, head_dim)),
        ],
        1,
    )
    projected = jnp.dot(normed, w_key_value, preferred_element_type=jnp.float32)
    keyval = jnp.concatenate(
        [rotate(projected[:, :head_dim], positions), projected[:, head_dim:]], 1
    ).astype(jnp.bfloat16)
    reach = WINDOW // row_count
    blocks = [keyval] + [passed_along(keyval, "seq", hop) for hop in range(1, reach + 1)]
    ordered = blocks[::-1]
    attn_out = attend(queries, table, ordered, w_out, reach * row_count)
    page_count = row_count // PAGE
    pages = keyval.reshape(page_count, PAGE, 2 * head_dim)
    pages = jnp.concatenate([pages, jnp.zeros((1, PAGE, 2 * head_dim), pages.dtype)], 0)
    page_index = jnp.arange(page_count, dtype=jnp.int32)[:, None]
    pick = jnp.sum(jnp.where(owner_hits, page_index, 0), 0)
    pick = jnp.where(jnp.any(owner_hits, 0), pick, page_count)
    got = lax.all_to_all(pages[pick], "seq", split_axis=0, concat_axis=0, tiled=True)
    got = jnp.concatenate([got, jnp.zeros((1, PAGE, 2 * head_dim), got.dtype)], 0)
    landed = heard[:, 2][None, :] == source[:, None] + 1
    from_source = jnp.sum(jnp.where(landed, source[None, :], 0), 1)
    from_source = jnp.where(jnp.any(landed, 1), from_source, devices)
    cache = got[from_source]
    return (attn_out, cache.reshape(devices * PAGE, 2 * head_dim))


def solution(mesh):
    placed = (P("seq", None), P(), P(), P(), P(), P("seq"), P("seq"), P("seq"))
    return jax.shard_map(
        layer,
        mesh=mesh,
        in_specs=placed,
        out_specs=(P("seq", None), P("seq", None)),
        check_vma=False,
    )
```

```python
import functools

import jax
import jax.numpy as jnp
from jax import lax
from jax.sharding import PartitionSpec as P
from jax.experimental import pallas as pl
from jax.experimental.pallas import tpu as pltpu

WINDOW = 1024
PAGE = 16


EPS = 1e-06
ROPE_BASE = 10000.0


def passed_along(value, axis, by):
    size = lax.axis_size(axis)
    pairs = [(i, i + by) for i in range(size) if 0 <= i + by < size]
    return lax.ppermute(value, axis, pairs)


def rotate(vectors, positions):
    width = vectors.shape[-1]
    half_dim = width // 2
    pair_index = jnp.arange(half_dim, dtype=jnp.float32)
    frequency = ROPE_BASE ** (-2.0 * pair_index / width)
    angles = positions.astype(jnp.float32)[:, None] * frequency[None, :]
    if vectors.ndim == 3:
        angles = angles[:, None, :]
    cosine = jnp.cos(angles)
    sine_part = jnp.sin(angles)
    first_half = vectors[..., :half_dim]
    second_half = vectors[..., half_dim:]
    return jnp.concatenate(
        [
            first_half * cosine - second_half * sine_part,
            second_half * cosine + first_half * sine_part,
        ],
        -1,
    )


def attend_kernel(
    query_ref,
    table_ref,
    early_ref,
    middle_ref,
    own_ref,
    weight_ref,
    out_ref,
    rows_ref,
    bias_ref,
    scores_ref,
    *,
    tile,
    back,
    head_count,
    head_dim,
    chunk,
):
    step = pl.program_id(0)
    block = own_ref.shape[0]

    @pl.when(step == 0)
    def _():
        rows_ref[0:block, :] = early_ref[...]
        rows_ref[block : 2 * block, :] = middle_ref[...]
        rows_ref[2 * block : 3 * block, :] = own_ref[...]

    span = tile + WINDOW
    key_first = pl.multiple_of(step * tile + back - WINDOW, tile)
    rows = rows_ref[pl.ds(key_first, span), :]
    keys = rows[:, :head_dim]
    values = rows[:, head_dim:]
    cosine = table_ref[:, 0:head_dim]
    sine_part = table_ref[:, head_dim : 2 * head_dim]
    first = table_ref[:, 2 * head_dim : 2 * head_dim + 1].astype(jnp.int32)
    query_at = step * tile + lax.broadcasted_iota(jnp.int32, (tile, span), 0)
    key_at = key_first - back + lax.broadcasted_iota(jnp.int32, (tile, span), 1)
    valid = (key_at >= first) & (key_at <= query_at) & (query_at - key_at < WINDOW)
    bias_ref[...] = jnp.where(valid, 0.0, -1e30).astype(jnp.float32)
    pieces = []
    for head in range(head_count):
        vectors = query_ref[:, head * head_dim : (head + 1) * head_dim]
        swapped = pltpu.roll(vectors, head_dim // 2, 1)
        turned = vectors * cosine + swapped * sine_part
        pieces.append((turned * head_dim ** (-0.5)).astype(jnp.bfloat16))
    stacked = jnp.concatenate(pieces, 0)
    scores_ref[...] = lax.dot_general(
        stacked, keys, (((1,), (1,)), ((), ())), preferred_element_type=jnp.float32
    )
    for head in range(head_count):
        for part in range(tile // chunk):
            row = head * tile + part * chunk
            scores = scores_ref[row : row + chunk, :] + bias_ref[part * chunk : (part + 1) * chunk, :]
            peak = jnp.max(scores, 1, keepdims=True)
            exponent = jnp.exp(scores - peak)
            probs = exponent / jnp.sum(exponent, 1, keepdims=True)
            scores_ref[row : row + chunk, :] = probs
    context = jnp.dot(
        scores_ref[...].astype(jnp.bfloat16), values, preferred_element_type=jnp.float32
    )
    context = jnp.concatenate(
        [
            context[head * tile : (head + 1) * tile].astype(jnp.bfloat16)
            for head in range(head_count)
        ],
        1,
    )
    out_ref[...] = jnp.dot(
        context, weight_ref[...], preferred_element_type=jnp.float32
    ).astype(out_ref.dtype)


def attend(projected, table, blocks, weight, back, tile=128, chunk=32):
    row_count, width = projected.shape
    head_dim = blocks[0].shape[1] // 2
    kernel = functools.partial(
        attend_kernel,
        tile=tile,
        back=back,
        head_count=width // head_dim,
        head_dim=head_dim,
        chunk=chunk,
    )
    whole = pl.BlockSpec(blocks[0].shape, lambda i: (0, 0))
    return pl.pallas_call(
        kernel,
        grid=(row_count // tile,),
        in_specs=[
            pl.BlockSpec((tile, width), lambda i: (i, 0)),
            pl.BlockSpec((tile, table.shape[1]), lambda i: (i, 0)),
            whole,
            whole,
            whole,
            pl.BlockSpec(weight.shape, lambda i: (0, 0)),
        ],
        out_specs=pl.BlockSpec((tile, weight.shape[1]), lambda i: (i, 0)),
        out_shape=jax.ShapeDtypeStruct((row_count, weight.shape[1]), jnp.bfloat16),
        scratch_shapes=[
            pltpu.VMEM((len(blocks) * row_count, 2 * head_dim), blocks[0].dtype),
            pltpu.VMEM((tile, tile + WINDOW), jnp.float32),
            pltpu.VMEM((width // head_dim * tile, tile + WINDOW), jnp.float32),
        ],
        compiler_params=pltpu.CompilerParams(vmem_limit_bytes=60 * 1024 * 1024),
    )(projected, table, *blocks, weight)


def layer(tokens, norm_gain, w_query, w_key_value, w_out, segment_ids, page_owner, page_slot):
    row_count = tokens.shape[0]
    devices = lax.axis_size("seq")
    offset = lax.axis_index("seq") * row_count
    head_dim = w_key_value.shape[1] // 2
    local_index = jnp.arange(row_count, dtype=jnp.int32)
    global_index = offset + local_index
    local_start = jnp.sum((segment_ids[None, :] < segment_ids[:, None]).astype(jnp.int32), 1)
    place = lax.axis_index("seq")
    page_count = row_count // PAGE
    row = jnp.concatenate(
        [segment_ids, page_owner, page_slot, jnp.zeros((128 - 2 * page_count,), jnp.int32)]
    )
    notes = jnp.broadcast_to(row[None, :], (devices, row.shape[0]))
    heard = lax.all_to_all(notes, "seq", split_axis=0, concat_axis=0, tiled=True)
    owner_hits = page_owner[:, None] == jnp.arange(devices, dtype=jnp.int32)[None, :]
    source = jnp.arange(devices, dtype=jnp.int32)
    every_id = heard[:, :row_count]
    owned_here = heard[:, row_count : row_count + page_count] == place
    slot_from = jnp.sum(
        jnp.where(owned_here, heard[:, row_count + page_count : row_count + 2 * page_count] + 1, 0), 1
    )
    prior_id = jnp.where(place >= 1, every_id[jnp.maximum(place - 1, 0), row_count - 1], -1)
    prior_first = jnp.sum((every_id < prior_id).astype(jnp.int32))
    starts = jnp.where(segment_ids == prior_id, prior_first, offset + local_start)
    positions = global_index - starts
    wide = tokens.astype(jnp.float32)
    mean_square = jnp.mean(wide * wide, -1, keepdims=True)
    normed = (wide * lax.rsqrt(mean_square + EPS) * norm_gain).astype(jnp.bfloat16)
    queries = jnp.dot(normed, w_query, preferred_element_type=jnp.float32)
    pair_index = jnp.arange(head_dim // 2, dtype=jnp.float32)
    frequency = ROPE_BASE ** (-2.0 * pair_index / head_dim)
    angles = positions.astype(jnp.float32)[:, None] * frequency[None, :]
    table = jnp.concatenate(
        [
            jnp.cos(angles),
            jnp.cos(angles),
            -jnp.sin(angles),
            jnp.sin(angles),
            jnp.broadcast_to((starts - offset).astype(jnp.float32)[:, None], (row_count, head_dim)),
        ],
        1,
    )
    projected = jnp.dot(normed, w_key_value, preferred_element_type=jnp.float32)
    keyval = jnp.concatenate(
        [rotate(projected[:, :head_dim], positions), projected[:, head_dim:]], 1
    ).astype(jnp.bfloat16)
    reach = WINDOW // row_count
    blocks = [keyval] + [passed_along(keyval, "seq", hop) for hop in range(1, reach + 1)]
    ordered = blocks[::-1]
    attn_out = attend(queries, table, ordered, w_out, reach * row_count)
    pages = keyval.reshape(page_count, PAGE, 2 * head_dim)
    pages = jnp.concatenate([pages, jnp.zeros((1, PAGE, 2 * head_dim), pages.dtype)], 0)
    page_index = jnp.arange(page_count, dtype=jnp.int32)[:, None]
    pick = jnp.sum(jnp.where(owner_hits, page_index, 0), 0)
    pick = jnp.where(jnp.any(owner_hits, 0), pick, page_count)
    got = lax.all_to_all(pages[pick], "seq", split_axis=0, concat_axis=0, tiled=True)
    got = jnp.concatenate([got, jnp.zeros((1, PAGE, 2 * head_dim), got.dtype)], 0)
    landed = slot_from[None, :] == source[:, None] + 1
    from_source = jnp.sum(jnp.where(landed, source[None, :], 0), 1)
    from_source = jnp.where(jnp.any(landed, 1), from_source, devices)
    cache = got[from_source]
    return (attn_out, cache.reshape(devices * PAGE, 2 * head_dim))


def solution(mesh):
    placed = (P("seq", None), P(), P(), P(), P(), P("seq"), P("seq"), P("seq"))
    return jax.shard_map(
        layer,
        mesh=mesh,
        in_specs=placed,
        out_specs=(P("seq", None), P("seq", None)),
        check_vma=False,
    )
```

```python
import functools

import jax
import jax.numpy as jnp
from jax import lax
from jax.sharding import PartitionSpec as P
from jax.experimental import pallas as pl
from jax.experimental.pallas import tpu as pltpu

WINDOW = 1024
PAGE = 16


EPS = 1e-06
ROPE_BASE = 10000.0


def passed_along(value, axis, by):
    size = lax.axis_size(axis)
    pairs = [(i, i + by) for i in range(size) if 0 <= i + by < size]
    return lax.ppermute(value, axis, pairs)


def rotate(vectors, positions):
    width = vectors.shape[-1]
    half_dim = width // 2
    pair_index = jnp.arange(half_dim, dtype=jnp.float32)
    frequency = ROPE_BASE ** (-2.0 * pair_index / width)
    angles = positions.astype(jnp.float32)[:, None] * frequency[None, :]
    if vectors.ndim == 3:
        angles = angles[:, None, :]
    cosine = jnp.cos(angles)
    sine_part = jnp.sin(angles)
    first_half = vectors[..., :half_dim]
    second_half = vectors[..., half_dim:]
    return jnp.concatenate(
        [
            first_half * cosine - second_half * sine_part,
            second_half * cosine + first_half * sine_part,
        ],
        -1,
    )


def attend_kernel(
    query_ref,
    table_ref,
    early_ref,
    middle_ref,
    own_ref,
    weight_ref,
    out_ref,
    rows_ref,
    bias_ref,
    scores_ref,
    probs_ref,
    *,
    tile,
    back,
    head_count,
    head_dim,
    chunk,
):
    step = pl.program_id(0)
    block = own_ref.shape[0]

    @pl.when(step == 0)
    def _():
        rows_ref[0:block, :] = early_ref[...]
        rows_ref[block : 2 * block, :] = middle_ref[...]
        rows_ref[2 * block : 3 * block, :] = own_ref[...]

    span = tile + WINDOW
    key_first = pl.multiple_of(step * tile + back - WINDOW, tile)
    rows = rows_ref[pl.ds(key_first, span), :]
    keys = rows[:, :head_dim]
    values = rows[:, head_dim:]
    cosine = table_ref[:, 0:head_dim]
    sine_part = table_ref[:, head_dim : 2 * head_dim]
    first = table_ref[:, 2 * head_dim : 2 * head_dim + 1].astype(jnp.int32)
    query_at = step * tile + lax.broadcasted_iota(jnp.int32, (tile, span), 0)
    key_at = key_first - back + lax.broadcasted_iota(jnp.int32, (tile, span), 1)
    valid = (key_at >= first) & (key_at <= query_at) & (query_at - key_at < WINDOW)
    bias_ref[...] = jnp.where(valid, 0.0, -1e30).astype(jnp.float32)
    pieces = []
    for head in range(head_count):
        vectors = query_ref[:, head * head_dim : (head + 1) * head_dim]
        swapped = pltpu.roll(vectors, head_dim // 2, 1)
        turned = vectors * cosine + swapped * sine_part
        pieces.append((turned * head_dim ** (-0.5)).astype(jnp.bfloat16))
    stacked = jnp.concatenate(pieces, 0)
    scores_ref[...] = lax.dot_general(
        stacked, keys, (((1,), (1,)), ((), ())), preferred_element_type=jnp.float32
    )
    for head in range(head_count):
        for part in range(tile // chunk):
            row = head * tile + part * chunk
            scores = scores_ref[row : row + chunk, :] + bias_ref[part * chunk : (part + 1) * chunk, :]
            peak = jnp.max(scores, 1, keepdims=True)
            exponent = jnp.exp(scores - peak)
            probs = exponent / jnp.sum(exponent, 1, keepdims=True)
            probs_ref[row : row + chunk, :] = probs.astype(jnp.bfloat16)
    context = jnp.dot(probs_ref[...], values, preferred_element_type=jnp.float32)
    context = jnp.concatenate(
        [
            context[head * tile : (head + 1) * tile].astype(jnp.bfloat16)
            for head in range(head_count)
        ],
        1,
    )
    out_ref[...] = jnp.dot(
        context, weight_ref[...], preferred_element_type=jnp.float32
    ).astype(out_ref.dtype)


def attend(projected, table, blocks, weight, back, tile=128, chunk=32):
    row_count, width = projected.shape
    head_dim = blocks[0].shape[1] // 2
    kernel = functools.partial(
        attend_kernel,
        tile=tile,
        back=back,
        head_count=width // head_dim,
        head_dim=head_dim,
        chunk=chunk,
    )
    whole = pl.BlockSpec(blocks[0].shape, lambda i: (0, 0))
    return pl.pallas_call(
        kernel,
        grid=(row_count // tile,),
        in_specs=[
            pl.BlockSpec((tile, width), lambda i: (i, 0)),
            pl.BlockSpec((tile, table.shape[1]), lambda i: (i, 0)),
            whole,
            whole,
            whole,
            pl.BlockSpec(weight.shape, lambda i: (0, 0)),
        ],
        out_specs=pl.BlockSpec((tile, weight.shape[1]), lambda i: (i, 0)),
        out_shape=jax.ShapeDtypeStruct((row_count, weight.shape[1]), jnp.bfloat16),
        scratch_shapes=[
            pltpu.VMEM((len(blocks) * row_count, 2 * head_dim), blocks[0].dtype),
            pltpu.VMEM((tile, tile + WINDOW), jnp.float32),
            pltpu.VMEM((width // head_dim * tile, tile + WINDOW), jnp.float32),
            pltpu.VMEM((width // head_dim * tile, tile + WINDOW), jnp.bfloat16),
        ],
        compiler_params=pltpu.CompilerParams(vmem_limit_bytes=60 * 1024 * 1024),
    )(projected, table, *blocks, weight)


def layer(tokens, norm_gain, w_query, w_key_value, w_out, segment_ids, page_owner, page_slot):
    row_count = tokens.shape[0]
    devices = lax.axis_size("seq")
    offset = lax.axis_index("seq") * row_count
    head_dim = w_key_value.shape[1] // 2
    local_index = jnp.arange(row_count, dtype=jnp.int32)
    global_index = offset + local_index
    local_start = jnp.sum((segment_ids[None, :] < segment_ids[:, None]).astype(jnp.int32), 1)
    place = lax.axis_index("seq")
    owner_hits = page_owner[:, None] == jnp.arange(devices, dtype=jnp.int32)[None, :]
    slot_to = jnp.sum(jnp.where(owner_hits, page_slot[:, None] + 1, 0), 0)
    notes = jnp.concatenate(
        [
            jnp.broadcast_to(segment_ids[None, :], (devices, row_count)),
            jnp.broadcast_to(slot_to[:, None], (devices, 128)),
        ],
        1,
    )
    heard = lax.all_to_all(notes, "seq", split_axis=0, concat_axis=0, tiled=True)
    source = jnp.arange(devices, dtype=jnp.int32)
    every_id = heard[:, :row_count]
    slot_from = heard[:, row_count]
    prior_id = jnp.where(place >= 1, every_id[jnp.maximum(place - 1, 0), row_count - 1], -1)
    prior_first = jnp.sum((every_id < prior_id).astype(jnp.int32))
    starts = jnp.where(segment_ids == prior_id, prior_first, offset + local_start)
    positions = global_index - starts
    wide = tokens.astype(jnp.float32)
    mean_square = jnp.mean(wide * wide, -1, keepdims=True)
    normed = (wide * lax.rsqrt(mean_square + EPS) * norm_gain).astype(jnp.bfloat16)
    queries = jnp.dot(normed, w_query, preferred_element_type=jnp.float32)
    pair_index = jnp.arange(head_dim // 2, dtype=jnp.float32)
    frequency = ROPE_BASE ** (-2.0 * pair_index / head_dim)
    angles = positions.astype(jnp.float32)[:, None] * frequency[None, :]
    table = jnp.concatenate(
        [
            jnp.cos(angles),
            jnp.cos(angles),
            -jnp.sin(angles),
            jnp.sin(angles),
            jnp.broadcast_to((starts - offset).astype(jnp.float32)[:, None], (row_count, head_dim)),
        ],
        1,
    )
    projected = jnp.dot(normed, w_key_value, preferred_element_type=jnp.float32)
    keyval = jnp.concatenate(
        [rotate(projected[:, :head_dim], positions), projected[:, head_dim:]], 1
    ).astype(jnp.bfloat16)
    reach = WINDOW // row_count
    blocks = [keyval] + [passed_along(keyval, "seq", hop) for hop in range(1, reach + 1)]
    ordered = blocks[::-1]
    attn_out = attend(queries, table, ordered, w_out, reach * row_count)
    page_count = row_count // PAGE
    pages = keyval.reshape(page_count, PAGE, 2 * head_dim)
    pages = jnp.concatenate([pages, jnp.zeros((1, PAGE, 2 * head_dim), pages.dtype)], 0)
    page_index = jnp.arange(page_count, dtype=jnp.int32)[:, None]
    pick = jnp.sum(jnp.where(owner_hits, page_index, 0), 0)
    pick = jnp.where(jnp.any(owner_hits, 0), pick, page_count)
    got = lax.all_to_all(pages[pick], "seq", split_axis=0, concat_axis=0, tiled=True)
    got = jnp.concatenate([got, jnp.zeros((1, PAGE, 2 * head_dim), got.dtype)], 0)
    landed = slot_from[None, :] == source[:, None] + 1
    from_source = jnp.sum(jnp.where(landed, source[None, :], 0), 1)
    from_source = jnp.where(jnp.any(landed, 1), from_source, devices)
    cache = got[from_source]
    return (attn_out, cache.reshape(devices * PAGE, 2 * head_dim))


def solution(mesh):
    placed = (P("seq", None), P(), P(), P(), P(), P("seq"), P("seq"), P("seq"))
    return jax.shard_map(
        layer,
        mesh=mesh,
        in_specs=placed,
        out_specs=(P("seq", None), P("seq", None)),
        check_vma=False,
    )
```

```python
import functools

import jax
import jax.numpy as jnp
from jax import lax
from jax.sharding import PartitionSpec as P
from jax.experimental import pallas as pl
from jax.experimental.pallas import tpu as pltpu

WINDOW = 1024
PAGE = 16


EPS = 1e-06
ROPE_BASE = 10000.0


def passed_along(value, axis, by):
    size = lax.axis_size(axis)
    pairs = [(i, i + by) for i in range(size) if 0 <= i + by < size]
    return lax.ppermute(value, axis, pairs)


def rotate(vectors, positions):
    width = vectors.shape[-1]
    half_dim = width // 2
    pair_index = jnp.arange(half_dim, dtype=jnp.float32)
    frequency = ROPE_BASE ** (-2.0 * pair_index / width)
    angles = positions.astype(jnp.float32)[:, None] * frequency[None, :]
    if vectors.ndim == 3:
        angles = angles[:, None, :]
    cosine = jnp.cos(angles)
    sine_part = jnp.sin(angles)
    first_half = vectors[..., :half_dim]
    second_half = vectors[..., half_dim:]
    return jnp.concatenate(
        [
            first_half * cosine - second_half * sine_part,
            second_half * cosine + first_half * sine_part,
        ],
        -1,
    )


def attend_kernel(
    query_ref,
    table_ref,
    early_ref,
    middle_ref,
    own_ref,
    weight_ref,
    out_ref,
    rows_ref,
    bias_ref,
    scores_ref,
    *,
    tile,
    back,
    head_count,
    head_dim,
    chunk,
):
    step = pl.program_id(0)
    block = own_ref.shape[0]

    @pl.when(step == 0)
    def _():
        rows_ref[0:block, :] = early_ref[...]
        rows_ref[block : 2 * block, :] = middle_ref[...]
        rows_ref[2 * block : 3 * block, :] = own_ref[...]

    span = tile + WINDOW
    key_first = pl.multiple_of(step * tile + back - WINDOW, tile)
    rows = rows_ref[pl.ds(key_first, span), :]
    keys = rows[:, :head_dim]
    values = rows[:, head_dim:]
    cosine = table_ref[:, 0:head_dim]
    sine_part = table_ref[:, head_dim : 2 * head_dim]
    first = table_ref[:, 2 * head_dim : 2 * head_dim + 1].astype(jnp.int32)
    query_at = step * tile + lax.broadcasted_iota(jnp.int32, (tile, span), 0)
    key_at = key_first - back + lax.broadcasted_iota(jnp.int32, (tile, span), 1)
    valid = (key_at >= first) & (key_at <= query_at) & (query_at - key_at < WINDOW)
    bias_ref[...] = jnp.where(valid, 0.0, -1e30).astype(jnp.float32)
    pieces = []
    for head in range(head_count):
        vectors = query_ref[:, head * head_dim : (head + 1) * head_dim]
        swapped = pltpu.roll(vectors, head_dim // 2, 1)
        turned = vectors * cosine + swapped * sine_part
        pieces.append((turned * head_dim ** (-0.5)).astype(jnp.bfloat16))
    stacked = jnp.concatenate(pieces, 0)
    scores_ref[...] = lax.dot_general(
        stacked, keys, (((1,), (1,)), ((), ())), preferred_element_type=jnp.float32
    )
    for head in range(head_count):
        for part in range(tile // chunk):
            row = head * tile + part * chunk
            scores = scores_ref[row : row + chunk, :] + bias_ref[part * chunk : (part + 1) * chunk, :]
            peak = jnp.max(scores, 1, keepdims=True)
            exponent = jnp.exp(scores - peak)
            probs = exponent / jnp.sum(exponent, 1, keepdims=True)
            scores_ref[row : row + chunk, :] = probs
    context = jnp.dot(
        scores_ref[...].astype(jnp.bfloat16), values, preferred_element_type=jnp.float32
    )
    context = jnp.concatenate(
        [
            context[head * tile : (head + 1) * tile].astype(jnp.bfloat16)
            for head in range(head_count)
        ],
        1,
    )
    out_ref[...] = jnp.dot(
        context, weight_ref[...], preferred_element_type=jnp.float32
    ).astype(out_ref.dtype)


def attend(projected, table, blocks, weight, back, tile=64, chunk=32):
    row_count, width = projected.shape
    head_dim = blocks[0].shape[1] // 2
    kernel = functools.partial(
        attend_kernel,
        tile=tile,
        back=back,
        head_count=width // head_dim,
        head_dim=head_dim,
        chunk=chunk,
    )
    whole = pl.BlockSpec(blocks[0].shape, lambda i: (0, 0))
    return pl.pallas_call(
        kernel,
        grid=(row_count // tile,),
        in_specs=[
            pl.BlockSpec((tile, width), lambda i: (i, 0)),
            pl.BlockSpec((tile, table.shape[1]), lambda i: (i, 0)),
            whole,
            whole,
            whole,
            pl.BlockSpec(weight.shape, lambda i: (0, 0)),
        ],
        out_specs=pl.BlockSpec((tile, weight.shape[1]), lambda i: (i, 0)),
        out_shape=jax.ShapeDtypeStruct((row_count, weight.shape[1]), jnp.bfloat16),
        scratch_shapes=[
            pltpu.VMEM((len(blocks) * row_count, 2 * head_dim), blocks[0].dtype),
            pltpu.VMEM((tile, tile + WINDOW), jnp.float32),
            pltpu.VMEM((width // head_dim * tile, tile + WINDOW), jnp.float32),
        ],
        compiler_params=pltpu.CompilerParams(vmem_limit_bytes=60 * 1024 * 1024),
    )(projected, table, *blocks, weight)


def layer(tokens, norm_gain, w_query, w_key_value, w_out, segment_ids, page_owner, page_slot):
    row_count = tokens.shape[0]
    devices = lax.axis_size("seq")
    offset = lax.axis_index("seq") * row_count
    head_dim = w_key_value.shape[1] // 2
    local_index = jnp.arange(row_count, dtype=jnp.int32)
    global_index = offset + local_index
    local_start = jnp.sum((segment_ids[None, :] < segment_ids[:, None]).astype(jnp.int32), 1)
    place = lax.axis_index("seq")
    owner_hits = page_owner[:, None] == jnp.arange(devices, dtype=jnp.int32)[None, :]
    slot_to = jnp.sum(jnp.where(owner_hits, page_slot[:, None] + 1, 0), 0)
    notes = jnp.concatenate(
        [
            jnp.broadcast_to(segment_ids[None, :], (devices, row_count)),
            jnp.broadcast_to(slot_to[:, None], (devices, 128)),
        ],
        1,
    )
    heard = lax.all_to_all(notes, "seq", split_axis=0, concat_axis=0, tiled=True)
    source = jnp.arange(devices, dtype=jnp.int32)
    every_id = heard[:, :row_count]
    slot_from = heard[:, row_count]
    prior_id = jnp.where(place >= 1, every_id[jnp.maximum(place - 1, 0), row_count - 1], -1)
    prior_first = jnp.sum((every_id < prior_id).astype(jnp.int32))
    starts = jnp.where(segment_ids == prior_id, prior_first, offset + local_start)
    positions = global_index - starts
    wide = tokens.astype(jnp.float32)
    mean_square = jnp.mean(wide * wide, -1, keepdims=True)
    normed = (wide * lax.rsqrt(mean_square + EPS) * norm_gain).astype(jnp.bfloat16)
    queries = jnp.dot(normed, w_query, preferred_element_type=jnp.float32)
    pair_index = jnp.arange(head_dim // 2, dtype=jnp.float32)
    frequency = ROPE_BASE ** (-2.0 * pair_index / head_dim)
    angles = positions.astype(jnp.float32)[:, None] * frequency[None, :]
    table = jnp.concatenate(
        [
            jnp.cos(angles),
            jnp.cos(angles),
            -jnp.sin(angles),
            jnp.sin(angles),
            jnp.broadcast_to((starts - offset).astype(jnp.float32)[:, None], (row_count, head_dim)),
        ],
        1,
    )
    projected = jnp.dot(normed, w_key_value, preferred_element_type=jnp.float32)
    keyval = jnp.concatenate(
        [rotate(projected[:, :head_dim], positions), projected[:, head_dim:]], 1
    ).astype(jnp.bfloat16)
    reach = WINDOW // row_count
    blocks = [keyval] + [passed_along(keyval, "seq", hop) for hop in range(1, reach + 1)]
    ordered = blocks[::-1]
    attn_out = attend(queries, table, ordered, w_out, reach * row_count)
    page_count = row_count // PAGE
    pages = keyval.reshape(page_count, PAGE, 2 * head_dim)
    pages = jnp.concatenate([pages, jnp.zeros((1, PAGE, 2 * head_dim), pages.dtype)], 0)
    page_index = jnp.arange(page_count, dtype=jnp.int32)[:, None]
    pick = jnp.sum(jnp.where(owner_hits, page_index, 0), 0)
    pick = jnp.where(jnp.any(owner_hits, 0), pick, page_count)
    got = lax.all_to_all(pages[pick], "seq", split_axis=0, concat_axis=0, tiled=True)
    got = jnp.concatenate([got, jnp.zeros((1, PAGE, 2 * head_dim), got.dtype)], 0)
    landed = slot_from[None, :] == source[:, None] + 1
    from_source = jnp.sum(jnp.where(landed, source[None, :], 0), 1)
    from_source = jnp.where(jnp.any(landed, 1), from_source, devices)
    cache = got[from_source]
    return (attn_out, cache.reshape(devices * PAGE, 2 * head_dim))


def solution(mesh):
    placed = (P("seq", None), P(), P(), P(), P(), P("seq"), P("seq"), P("seq"))
    return jax.shard_map(
        layer,
        mesh=mesh,
        in_specs=placed,
        out_specs=(P("seq", None), P("seq", None)),
        check_vma=False,
    )
```
